256 devices in a mesh: gx: 8 (over x_lo, y), gy: 32 (over x_hi, z, core).
Axes of the slice: x: 4 (x_hi: 2, x_lo: 2; x = x_hi * 2 + x_lo), y: 4, z: 8, core: 2. Of those that a mesh axis runs over, the one named last changes fastest.
Arguments:
- source: bfloat16 [288, 8, 32, 1024], P(None, 'gx', 'gy'), may hold values from -6 to 6
- slope: float32 [2, 144], replicated, may hold values from -6 to 6
- quad: bfloat16 [4, 4, 2, 20736], replicated, may hold values from -1 to 1, as said below
- pair: bfloat16 [2, 2, 2, 20736], replicated, may hold values from -1 to 1, as said below
Outputs:
- image: bfloat16 [288, 8, 32, 1024], P(None, 'gx', 'gy')
The draws below stay inside these ranges and needn't reach their ends.
Inputs may be any that keep to these rules, and one draw needn't show every extreme that they name: `quad`: translation coefficients. `pair`: translation coefficients.
All inputs are finite; a program needn't handle non-finite values.
Results may differ from the reference program's by a relative error of at most 0.02.
Values may be sent and summed in bfloat16 or wider, within the bound.
No kernel may reach another device: no remote copies, remote signals or barrier semaphores. Data moves between devices by JAX's collectives and lax.ppermute only.
A program may use at most 64 MiB of HBM per device.

```python
import math
import jax
import jax.numpy as jnp

P_SIZE = 144
F = 288
SIDE = 32
BX = 256
BY = 1024
N_GX = 8
N_GY = 32


def draw_noise(key, shape):
    return jnp.clip(jax.random.normal(key, shape, jnp.float32), -4.0, 4.0)


def draw_quad(key, part):
    target = jnp.arange(4)[:, None]
    child = jnp.arange(4)[None, :]
    differ = (target // 2 != child // 2).astype(jnp.int32) + (target % 2 != child % 2).astype(jnp.int32)
    real_core = jnp.where(differ == 0, 0.5, jnp.where(differ == 2, -0.5, 0.0))
    imag_core = jnp.where(differ == 1, 0.5, 0.0)
    core = jnp.stack([real_core, imag_core], -1).astype(jnp.float32)
    identity = jnp.eye(P_SIZE, dtype=jnp.float32)
    base = core[:, :, :, None, None] * identity
    noise = draw_noise(key, (4, 4, 2, P_SIZE, P_SIZE))
    return (base + 0.175 / math.sqrt(P_SIZE) * noise).reshape(4, 4, 2, P_SIZE * P_SIZE).astype(jnp.bfloat16)


def draw_pair(key, part):
    target = jnp.arange(2)[:, None]
    child = jnp.arange(2)[None, :]
    same = target == child
    real_core = jnp.where(same, 0.70710678, 0.0)
    imag_core = jnp.where(same, 0.0, 0.70710678)
    core = jnp.stack([real_core, imag_core], -1).astype(jnp.float32)
    identity = jnp.eye(P_SIZE, dtype=jnp.float32)
    base = core[:, :, :, None, None] * identity
    noise = draw_noise(key, (2, 2, 2, P_SIZE, P_SIZE))
    return (base + 0.247 / math.sqrt(P_SIZE) * noise).reshape(2, 2, 2, P_SIZE * P_SIZE).astype(jnp.bfloat16)


def block_scale(own_key, dims, pieces, smallest, largest):
    level = 1.0
    for dim, blocks in pieces:
        steps = jax.random.uniform(jax.random.fold_in(jax.random.fold_in(own_key, 6), dim), (blocks,), jnp.float32, smallest / len(pieces), largest / len(pieces))
        level = level * jnp.repeat(jnp.exp(steps), dims[dim] // blocks).reshape((-1,) + (1,) * (len(dims) - 1 - dim))
    return level


def scatter_about(own_key, dims, deviation, most, shards=(), held_as=jnp.bfloat16):
    drawn = deviation * jax.random.normal(own_key, dims, jnp.float32)
    if shards:
        drawn = drawn * block_scale(own_key, dims, shards, -0.22, 0.18)
    return jnp.clip(drawn, -most, most).astype(held_as)


def setup_inputs(seed: int = 0) -> dict:
    arg_keys = jax.random.split(jax.random.key(seed), 5)
    source = scatter_about(arg_keys[0], (F, N_GX, N_GY, SIDE * SIDE), 1.0, 6.0, ((1, 8), (2, 32)))
    slope = jnp.clip(jax.random.uniform(arg_keys[1], (2, P_SIZE), jnp.float32, -6.0, 6.0), -6.0, 6.0)
    quad = draw_quad(jax.random.fold_in(arg_keys[4], 71), 0)
    pair = draw_pair(jax.random.fold_in(arg_keys[4], 71), 0)
    return {"source": source, "slope": slope, "quad": quad, "pair": pair}


def complex_block(coefficients):
    real_part = coefficients[..., 0, :, :]
    imag_part = coefficients[..., 1, :, :]
    upper_rows = jnp.concatenate([real_part, -imag_part], -1)
    lower_rows = jnp.concatenate([imag_part, real_part], -1)
    return jnp.concatenate([upper_rows, lower_rows], -2)


def translate(current, depth, x_live, quad_block, pair_block):
    width_all, boxes_x, boxes_y = current.shape
    split_x = 2 if x_live else 1
    inner_x = (1 << depth) if x_live else 1
    inner_y = 1 << depth
    shape_seven = (width_all, boxes_x // (split_x * inner_x), split_x, inner_x, boxes_y // (2 * inner_y), 2, inner_y)
    shaped = current.reshape(shape_seven)
    stacked_rows = []
    for slot_x in range(split_x):
        columns = []
        for slot_y in range(2):
            summed = None
            for step_x in range(split_x):
                for step_y in range(2):
                    child_x = (slot_x + step_x) % 2
                    child_y = (slot_y + step_y) % 2
                    block_rows = shaped[:, :, child_x if x_live else 0, :, :, child_y, :]
                    if x_live:
                        matrix = quad_block[slot_x * 2 + slot_y, child_x * 2 + child_y]
                    else:
                        matrix = pair_block[slot_y, child_y]
                    product_term = jnp.dot(matrix.astype(jnp.float32), block_rows.reshape(width_all, -1).astype(jnp.float32), preferred_element_type=jnp.float32)
                    summed = product_term if summed is None else summed + product_term
            columns.append(summed.reshape(block_rows.shape))
        stacked_rows.append(jnp.stack(columns, 4))
    return jnp.stack(stacked_rows, 2).reshape(width_all, boxes_x, boxes_y)


def reference(source, slope, quad, pair):
    width_all = source.shape[0]
    half_width = width_all // 2
    tiles_x = source.shape[1]
    tiles_y = source.shape[2]
    grid = source.reshape(width_all, tiles_x, tiles_y, SIDE, SIDE).transpose(0, 1, 3, 2, 4).reshape(width_all, BX, BY)
    quad_block = complex_block(quad.reshape(4, 4, 2, P_SIZE, P_SIZE))
    pair_block = complex_block(pair.reshape(2, 2, 2, P_SIZE, P_SIZE))
    bits_x = BX.bit_length() - 1
    bits_y = BY.bit_length() - 1
    center_x = (jnp.arange(BX).astype(jnp.float32) + 0.5) / float(BX) - 0.5
    center_y = (jnp.arange(BY).astype(jnp.float32) + 0.5) / float(BY) - 0.5
    angle = slope[0][:, None, None] * center_x[None, :, None] + slope[1][:, None, None] * center_y[None, None, :]
    cosine_table = jnp.cos(angle)
    sine_table = jnp.sin(angle)
    current = grid
    for depth in range(max(bits_x, bits_y)):
        merged = translate(current, depth, depth < bits_x, quad_block, pair_block)
        real_part = merged[:half_width]
        imag_part = merged[half_width:]
        current = jnp.concatenate([real_part * cosine_table - imag_part * sine_table, real_part * sine_table + imag_part * cosine_table], 0).astype(jnp.bfloat16)
    return current.reshape(width_all, tiles_x, SIDE, tiles_y, SIDE).transpose(0, 1, 3, 2, 4).reshape(width_all, tiles_x, tiles_y, SIDE * SIDE)
```

```python
import functools

import jax
import jax.numpy as jnp
from jax import lax
from jax.experimental import pallas as pl
from jax.experimental.pallas import tpu as pltpu
from jax.sharding import PartitionSpec as P

P_SIZE = 144
SIDE = 32
LANE = 256
WIDE = 2 * LANE


def padded(x):
    pad = [(0, 0)] * (x.ndim - 1) + [(0, LANE - P_SIZE)]
    return jnp.pad(x, pad).reshape(x.shape[:-2] + (WIDE,))


def weights(blocks):
    real = jnp.swapaxes(blocks[:, :, 0], -1, -2)
    imag = jnp.swapaxes(blocks[:, :, 1], -1, -2)
    upper = jnp.stack([real, imag], 2)
    lower = jnp.stack([-imag, real], 2)
    full = jnp.stack([upper, lower], 2)
    full = jnp.pad(full, [(0, 0)] * 4 + [(0, LANE - P_SIZE), (0, LANE - P_SIZE)])
    t, c = full.shape[:2]
    full = full.transpose(0, 1, 2, 4, 3, 5)
    return full.reshape(t, c * WIDE, WIDE)


def class_pieces(c, run, period, rows):
    if run >= 8:
        return [pl.ds(g * period + c * run, run) for g in range(rows // period)]
    return [pl.ds(c * run + k, rows // period, stride=period) for k in range(run)]


def load_class(ref, c, run, period):
    chunks, rows = ref.shape[:2]
    pieces = []
    for s in class_pieces(c, run, period, rows):
        parts = [ref[q, s, :] for q in range(chunks)]
        pieces.append(jnp.concatenate(parts, 1))
    return pieces[0] if len(pieces) == 1 else jnp.concatenate(pieces, 0)


def store_class(ref, c, run, period, value):
    chunks, rows = ref.shape[:2]
    at = 0
    for s in class_pieces(c, run, period, rows):
        size = s.size
        for q in range(chunks):
            ref[q, s, :] = value[at:at + size, q * 128:(q + 1) * 128]
        at += size


def levels_kernel(levels, x_ref, cos_ref, sin_ref, *refs):
    w_refs = refs[:-3]
    o_ref, s0, s1 = refs[-3:]
    for q in range(WIDE // 128):
        s0[q] = x_ref[:, q * 128:(q + 1) * 128].astype(jnp.float32)
    bufs = (s0, s1)
    for index, (kind, pos) in enumerate(levels):
        src = bufs[index % 2]
        dst = bufs[(index + 1) % 2]
        count = 4 if kind == "quad" else 2
        run = 1 << pos
        period = run * count
        w_ref = w_refs[0] if kind == "quad" else w_refs[-1]
        children = [load_class(src, c, run, period).astype(jnp.bfloat16) for c in range(count)]
        stacked = jnp.concatenate(children, 1)
        for t in range(count):
            y = jnp.dot(stacked, w_ref[t], preferred_element_type=jnp.float32)
            yr = y[:, :LANE]
            yi = y[:, LANE:]
            cs = load_class(cos_ref, t, run, period)
            sn = load_class(sin_ref, t, run, period)
            out_r = (yr * cs - yi * sn).astype(jnp.bfloat16).astype(jnp.float32)
            out_i = (yr * sn + yi * cs).astype(jnp.bfloat16).astype(jnp.float32)
            store_class(dst, t, run, period, jnp.concatenate([out_r, out_i], 1))
    last = bufs[len(levels) % 2]
    for q in range(WIDE // 128):
        o_ref[:, q * 128:(q + 1) * 128] = last[q].astype(o_ref.dtype)


def run_levels(levels, x, cos_t, sin_t, w_list):
    rows = x.shape[0]
    vmem = pl.BlockSpec(memory_space=pltpu.VMEM)
    return pl.pallas_call(
        functools.partial(levels_kernel, levels),
        out_shape=jax.ShapeDtypeStruct((rows, WIDE), jnp.bfloat16),
        in_specs=[vmem] * (3 + len(w_list)),
        out_specs=vmem,
        scratch_shapes=[pltpu.VMEM((WIDE // 128, rows, 128), jnp.float32)] * 2,
        compiler_params=pltpu.CompilerParams(vmem_limit_bytes=60 * 1024 * 1024),
    )(x, cos_t, sin_t, *w_list)


def bits_of(value, count):
    return [(value >> k) & 1 for k in range(count)]


def tables(slope, a, b):
    center_x = (a.astype(jnp.float32) + 0.5) / 256.0 - 0.5
    center_y = (b.astype(jnp.float32) + 0.5) / 1024.0 - 0.5
    angle = slope[0][None, :] * center_x[:, None] + slope[1][None, :] * center_y[:, None]
    pad = [(0, 0), (0, LANE - P_SIZE)]

    def chunked(v):
        return jnp.pad(v, pad).reshape(-1, LANE // 128, 128).transpose(1, 0, 2)

    return chunked(jnp.cos(angle)), chunked(jnp.sin(angle))


def local(source, slope, quad, pair):
    place_x = lax.axis_index("gx")
    place_y = lax.axis_index("gy")
    wq = weights(quad.reshape(4, 4, 2, P_SIZE, P_SIZE))
    wp = weights(pair.reshape(2, 2, 2, P_SIZE, P_SIZE))
    rows = jnp.arange(1024, dtype=jnp.int32)

    i1 = sum(((rows >> (2 * k + 1)) & 1) << k for k in range(5))
    j1 = sum(((rows >> (2 * k)) & 1) << k for k in range(5))
    cos1, sin1 = tables(slope, place_x * 32 + i1, place_y * 32 + j1)
    x = source.reshape(2, P_SIZE, 2, 2, 2, 2, 2, 2, 2, 2, 2, 2)
    x = x.transpose(2, 7, 3, 8, 4, 9, 5, 10, 6, 11, 0, 1).reshape(1024, 2, P_SIZE)
    y1 = run_levels([("quad", 2 * k) for k in range(5)], padded(x), cos1, sin1, [wq])

    z = y1.reshape(2, 2, 2, 2, 2, 2, 2, 2, 2, 2, 2, LANE)[..., :P_SIZE]
    z = z.transpose(4, 6, 8, 1, 3, 5, 7, 9, 0, 2, 10, 11).reshape(8, 32, 2, 2, 2, P_SIZE)
    z = lax.all_to_all(z, "gx", 0, 0, tiled=True)
    z = lax.all_to_all(z, "gy", 1, 1, tiled=True)
    z = z.reshape(2, 2, 2, 2, 2, 2, 2, 2, 2, 2, 2, P_SIZE)
    z = z.transpose(8, 9, 3, 4, 0, 5, 1, 6, 2, 7, 10, 11).reshape(1024, 2, P_SIZE)
    lo_a = bits_of(place_x, 3)
    lo_b = place_y
    r = [(rows >> k) & 1 for k in range(10)]
    a2 = lo_a[0] + 2 * lo_a[1] + 4 * lo_a[2] + 8 * r[8] + 16 * r[9] + 32 * r[1] + 64 * r[3] + 128 * r[5]
    b2 = lo_b + 32 * (r[0] + 2 * r[2] + 4 * r[4] + 8 * r[6] + 16 * r[7])
    cos2, sin2 = tables(slope, a2, b2)
    levels2 = [("quad", 0), ("quad", 2), ("quad", 4), ("pair", 6), ("pair", 7)]
    y2 = run_levels(levels2, padded(z), cos2, sin2, [wq, wp])

    w = y2.reshape(2, 2, 2, 2, 2, 2, 2, 2, 2, 2, 2, LANE)[..., :P_SIZE]
    w = w.transpose(4, 6, 8, 2, 3, 5, 7, 9, 0, 1, 10, 11).reshape(8, 32, 2, 2, 2, P_SIZE)
    w = lax.all_to_all(w, "gx", 0, 0, tiled=True)
    w = lax.all_to_all(w, "gy", 1, 1, tiled=True)
    w = w.reshape(2, 2, 2, 2, 2, 2, 2, 2, 2, 2, 2, P_SIZE)
    w = w.transpose(10, 11, 8, 9, 0, 1, 2, 3, 4, 5, 6, 7)
    return w.reshape(2 * P_SIZE, 1, 1, 1024)


def solution(mesh):
    in_specs = (P(None, "gx", "gy", None), P(), P(), P())
    out_specs = P(None, "gx", "gy", None)
    return jax.shard_map(local, mesh=mesh, in_specs=in_specs, out_specs=out_specs, check_vma=False)
```

```python
import functools

import jax
import jax.numpy as jnp
from jax import lax
from jax.experimental import pallas as pl
from jax.experimental.pallas import tpu as pltpu
from jax.sharding import PartitionSpec as P

P_SIZE = 144
SIDE = 32
LANE = 256
WIDE = 2 * LANE


def padded(x):
    pad = [(0, 0)] * (x.ndim - 1) + [(0, LANE - P_SIZE)]
    return jnp.pad(x, pad).reshape(x.shape[:-2] + (WIDE,))


def build_weights(wt_ref, m_ref):
    count = wt_ref.shape[0]
    for t in range(count):
        wt_ref[t] = jnp.zeros(wt_ref.shape[1:], wt_ref.dtype)
    for t in range(count):
        for c in range(count):
            real = m_ref[t, c, 0]
            imag = m_ref[t, c, 1]
            base = c * WIDE
            wt_ref[t, 0:P_SIZE, base:base + P_SIZE] = real
            wt_ref[t, 0:P_SIZE, base + LANE:base + LANE + P_SIZE] = -imag
            wt_ref[t, LANE:LANE + P_SIZE, base:base + P_SIZE] = imag
            wt_ref[t, LANE:LANE + P_SIZE, base + LANE:base + LANE + P_SIZE] = real


def class_pieces(c, run, period, rows):
    if run >= 8:
        return [pl.ds(g * period + c * run, run) for g in range(rows // period)]
    return [pl.ds(c * run + k, rows // period, stride=period) for k in range(run)]


def load_class(ref, c, run, period):
    chunks, rows = ref.shape[:2]
    pieces = []
    for s in class_pieces(c, run, period, rows):
        parts = [ref[q, s, :] for q in range(chunks)]
        pieces.append(jnp.concatenate(parts, 1))
    return pieces[0] if len(pieces) == 1 else jnp.concatenate(pieces, 0)


def store_class(ref, c, run, period, value):
    chunks, rows = ref.shape[:2]
    at = 0
    for s in class_pieces(c, run, period, rows):
        size = s.size
        for q in range(chunks):
            ref[q, s, :] = value[at:at + size, q * 128:(q + 1) * 128]
        at += size


def levels_kernel(levels, x_ref, cos_ref, sin_ref, *refs):
    count_w = (len(refs) - 3) // 2
    m_refs = refs[:count_w]
    o_ref, s0, s1 = refs[count_w:count_w + 3]
    w_refs = refs[count_w + 3:]
    for w_ref, m_ref in zip(w_refs, m_refs):
        build_weights(w_ref, m_ref)
    for q in range(WIDE // 128):
        s0[q] = x_ref[:, q * 128:(q + 1) * 128].astype(jnp.float32)
    bufs = (s0, s1)
    for index, (kind, pos) in enumerate(levels):
        src = bufs[index % 2]
        dst = bufs[(index + 1) % 2]
        count = 4 if kind == "quad" else 2
        run = 1 << pos
        period = run * count
        w_ref = w_refs[0] if kind == "quad" else w_refs[-1]
        children = [load_class(src, c, run, period).astype(jnp.bfloat16) for c in range(count)]
        stacked = jnp.concatenate(children, 1)
        for t in range(count):
            y = lax.dot_general(
                stacked, w_ref[t], (((1,), (1,)), ((), ())), preferred_element_type=jnp.float32
            )
            yr = y[:, :LANE]
            yi = y[:, LANE:]
            cs = load_class(cos_ref, t, run, period)
            sn = load_class(sin_ref, t, run, period)
            out_r = (yr * cs - yi * sn).astype(jnp.bfloat16).astype(jnp.float32)
            out_i = (yr * sn + yi * cs).astype(jnp.bfloat16).astype(jnp.float32)
            store_class(dst, t, run, period, jnp.concatenate([out_r, out_i], 1))
    last = bufs[len(levels) % 2]
    for q in range(WIDE // 128):
        o_ref[:, q * 128:(q + 1) * 128] = last[q].astype(o_ref.dtype)


def run_levels(levels, x, cos_t, sin_t, m_list):
    rows = x.shape[0]
    vmem = pl.BlockSpec(memory_space=pltpu.VMEM)
    w_scratch = [
        pltpu.VMEM((m.shape[0], WIDE, m.shape[1] * WIDE), jnp.bfloat16) for m in m_list
    ]
    return pl.pallas_call(
        functools.partial(levels_kernel, levels),
        out_shape=jax.ShapeDtypeStruct((rows, WIDE), jnp.bfloat16),
        in_specs=[vmem] * (3 + len(m_list)),
        out_specs=vmem,
        scratch_shapes=[pltpu.VMEM((WIDE // 128, rows, 128), jnp.float32)] * 2 + w_scratch,
        compiler_params=pltpu.CompilerParams(vmem_limit_bytes=60 * 1024 * 1024),
    )(x, cos_t, sin_t, *m_list)


def bits_of(value, count):
    return [(value >> k) & 1 for k in range(count)]


def tables(slope, a, b):
    center_x = (a.astype(jnp.float32) + 0.5) / 256.0 - 0.5
    center_y = (b.astype(jnp.float32) + 0.5) / 1024.0 - 0.5
    angle = slope[0][None, :] * center_x[:, None] + slope[1][None, :] * center_y[:, None]
    pad = [(0, 0), (0, LANE - P_SIZE)]

    def chunked(v):
        return jnp.pad(v, pad).reshape(-1, LANE // 128, 128).transpose(1, 0, 2)

    return chunked(jnp.cos(angle)), chunked(jnp.sin(angle))


def local(source, slope, quad, pair):
    place_x = lax.axis_index("gx")
    place_y = lax.axis_index("gy")
    wq = quad.reshape(4, 4, 2, P_SIZE, P_SIZE)
    wp = pair.reshape(2, 2, 2, P_SIZE, P_SIZE)
    rows = jnp.arange(1024, dtype=jnp.int32)

    i1 = sum(((rows >> (2 * k + 1)) & 1) << k for k in range(5))
    j1 = sum(((rows >> (2 * k)) & 1) << k for k in range(5))
    cos1, sin1 = tables(slope, place_x * 32 + i1, place_y * 32 + j1)
    x = source.reshape(2, P_SIZE, 2, 2, 2, 2, 2, 2, 2, 2, 2, 2)
    x = x.transpose(2, 7, 3, 8, 4, 9, 5, 10, 6, 11, 0, 1).reshape(1024, 2, P_SIZE)
    y1 = run_levels([("quad", 2 * k) for k in range(5)], padded(x), cos1, sin1, [wq])

    z = y1.reshape(2, 2, 2, 2, 2, 2, 2, 2, 2, 2, 2, LANE)[..., :P_SIZE]
    z = z.transpose(4, 6, 8, 1, 3, 5, 7, 9, 0, 2, 10, 11).reshape(8, 32, 2, 2, 2, P_SIZE)
    z = lax.all_to_all(z, "gx", 0, 0, tiled=True)
    z = lax.all_to_all(z, "gy", 1, 1, tiled=True)
    z = z.reshape(2, 2, 2, 2, 2, 2, 2, 2, 2, 2, 2, P_SIZE)
    z = z.transpose(8, 9, 3, 4, 0, 5, 1, 6, 2, 7, 10, 11).reshape(1024, 2, P_SIZE)
    lo_a = bits_of(place_x, 3)
    lo_b = place_y
    r = [(rows >> k) & 1 for k in range(10)]
    a2 = lo_a[0] + 2 * lo_a[1] + 4 * lo_a[2] + 8 * r[8] + 16 * r[9] + 32 * r[1] + 64 * r[3] + 128 * r[5]
    b2 = lo_b + 32 * (r[0] + 2 * r[2] + 4 * r[4] + 8 * r[6] + 16 * r[7])
    cos2, sin2 = tables(slope, a2, b2)
    levels2 = [("quad", 0), ("quad", 2), ("quad", 4), ("pair", 6), ("pair", 7)]
    y2 = run_levels(levels2, padded(z), cos2, sin2, [wq, wp])

    w = y2.reshape(2, 2, 2, 2, 2, 2, 2, 2, 2, 2, 2, LANE)[..., :P_SIZE]
    w = w.transpose(4, 6, 8, 2, 3, 5, 7, 9, 0, 1, 10, 11).reshape(8, 32, 2, 2, 2, P_SIZE)
    w = lax.all_to_all(w, "gx", 0, 0, tiled=True)
    w = lax.all_to_all(w, "gy", 1, 1, tiled=True)
    w = w.reshape(2, 2, 2, 2, 2, 2, 2, 2, 2, 2, 2, P_SIZE)
    w = w.transpose(10, 11, 8, 9, 0, 1, 2, 3, 4, 5, 6, 7)
    return w.reshape(2 * P_SIZE, 1, 1, 1024)


def solution(mesh):
    in_specs = (P(None, "gx", "gy", None), P(), P(), P())
    out_specs = P(None, "gx", "gy", None)
    return jax.shard_map(local, mesh=mesh, in_specs=in_specs, out_specs=out_specs, check_vma=False)
```

```python
import functools

import jax
import jax.numpy as jnp
from jax import lax
from jax.experimental import pallas as pl
from jax.experimental.pallas import tpu as pltpu
from jax.sharding import PartitionSpec as P

P_SIZE = 144
SIDE = 32
LANE = 256
WIDE = 2 * LANE


def padded(x):
    pad = [(0, 0)] * (x.ndim - 1) + [(0, LANE - P_SIZE)]
    return jnp.pad(x, pad).reshape(x.shape[:-2] + (WIDE,))


def build_weights(wt_ref, m_ref):
    count = wt_ref.shape[0]
    for t in range(count):
        wt_ref[t] = jnp.zeros(wt_ref.shape[1:], wt_ref.dtype)
    for t in range(count):
        for c in range(count):
            real = m_ref[t, c, 0]
            imag = m_ref[t, c, 1]
            base = c * WIDE
            wt_ref[t, 0:P_SIZE, base:base + P_SIZE] = real
            wt_ref[t, 0:P_SIZE, base + LANE:base + LANE + P_SIZE] = -imag
            wt_ref[t, LANE:LANE + P_SIZE, base:base + P_SIZE] = imag
            wt_ref[t, LANE:LANE + P_SIZE, base + LANE:base + LANE + P_SIZE] = real


def class_pieces(c, run, period, rows):
    if run >= 8:
        return [pl.ds(g * period + c * run, run) for g in range(rows // period)]
    return [pl.ds(c * run + k, rows // period, stride=period) for k in range(run)]


def load_class(ref, c, run, period):
    chunks, rows = ref.shape[:2]
    pieces = []
    for s in class_pieces(c, run, period, rows):
        parts = [ref[q, s, :] for q in range(chunks)]
        pieces.append(jnp.concatenate(parts, 1))
    return pieces[0] if len(pieces) == 1 else jnp.concatenate(pieces, 0)


def store_class(ref, c, run, period, value):
    chunks, rows = ref.shape[:2]
    at = 0
    for s in class_pieces(c, run, period, rows):
        size = s.size
        for q in range(chunks):
            ref[q, s, :] = value[at:at + size, q * 128:(q + 1) * 128]
        at += size


def levels_kernel(levels, x_ref, cos_ref, sin_ref, *refs):
    count_w = (len(refs) - 3) // 2
    m_refs = refs[:count_w]
    o_ref, s0, s1 = refs[count_w:count_w + 3]
    w_refs = refs[count_w + 3:]
    for w_ref, m_ref in zip(w_refs, m_refs):
        build_weights(w_ref, m_ref)
    for q in range(WIDE // 128):
        s0[q] = x_ref[:, q * 128:(q + 1) * 128].astype(jnp.float32)
    bufs = (s0, s1)
    for index, (kind, pos) in enumerate(levels):
        src = bufs[index % 2]
        dst = bufs[(index + 1) % 2]
        count = 4 if kind == "quad" else 2
        run = 1 << pos
        period = run * count
        w_ref = w_refs[0] if kind == "quad" else w_refs[-1]
        children = [load_class(src, c, run, period).astype(jnp.bfloat16) for c in range(count)]
        stacked = jnp.concatenate(children, 1)
        for t in range(count):
            y = lax.dot_general(
                stacked, w_ref[t], (((1,), (1,)), ((), ())), preferred_element_type=jnp.float32
            )
            yr = y[:, :LANE]
            yi = y[:, LANE:]
            cs = load_class(cos_ref, t, run, period)
            sn = load_class(sin_ref, t, run, period)
            out_r = (yr * cs - yi * sn).astype(jnp.bfloat16).astype(jnp.float32)
            out_i = (yr * sn + yi * cs).astype(jnp.bfloat16).astype(jnp.float32)
            store_class(dst, t, run, period, jnp.concatenate([out_r, out_i], 1))
    last = bufs[len(levels) % 2]
    for q in range(WIDE // 128):
        o_ref[:, q * 128:(q + 1) * 128] = last[q].astype(o_ref.dtype)


def run_levels(levels, x, cos_t, sin_t, m_list):
    rows = x.shape[0]
    vmem = pl.BlockSpec(memory_space=pltpu.VMEM)
    w_scratch = [
        pltpu.VMEM((m.shape[0], WIDE, m.shape[1] * WIDE), jnp.bfloat16) for m in m_list
    ]
    return pl.pallas_call(
        functools.partial(levels_kernel, levels),
        out_shape=jax.ShapeDtypeStruct((rows, WIDE), jnp.bfloat16),
        in_specs=[vmem] * (3 + len(m_list)),
        out_specs=vmem,
        scratch_shapes=[pltpu.VMEM((WIDE // 128, rows, 128), jnp.float32)] * 2 + w_scratch,
        compiler_params=pltpu.CompilerParams(vmem_limit_bytes=60 * 1024 * 1024),
    )(x, cos_t, sin_t, *m_list)


def bits_of(value, count):
    return [(value >> k) & 1 for k in range(count)]


def tables(slope, a, b):
    center_x = (a.astype(jnp.float32) + 0.5) / 256.0 - 0.5
    center_y = (b.astype(jnp.float32) + 0.5) / 1024.0 - 0.5
    angle = slope[0][None, :] * center_x[:, None] + slope[1][None, :] * center_y[:, None]
    pad = [(0, 0), (0, LANE - P_SIZE)]

    def chunked(v):
        return jnp.pad(v, pad).reshape(-1, LANE // 128, 128).transpose(1, 0, 2)

    return chunked(jnp.cos(angle)), chunked(jnp.sin(angle))


def exchange(z):
    shape = z.shape
    z = z.reshape((shape[0] * shape[1],) + shape[2:])
    z = lax.all_to_all(z, ("gx", "gy"), 0, 0, tiled=True)
    return z.reshape(shape)


def local(source, slope, quad, pair):
    place_x = lax.axis_index("gx")
    place_y = lax.axis_index("gy")
    wq = quad.reshape(4, 4, 2, P_SIZE, P_SIZE)
    wp = pair.reshape(2, 2, 2, P_SIZE, P_SIZE)
    rows = jnp.arange(1024, dtype=jnp.int32)

    i1 = sum(((rows >> (2 * k + 1)) & 1) << k for k in range(5))
    j1 = sum(((rows >> (2 * k)) & 1) << k for k in range(5))
    cos1, sin1 = tables(slope, place_x * 32 + i1, place_y * 32 + j1)
    x = source.reshape(2, P_SIZE, 2, 2, 2, 2, 2, 2, 2, 2, 2, 2)
    x = x.transpose(2, 7, 3, 8, 4, 9, 5, 10, 6, 11, 0, 1).reshape(1024, 2, P_SIZE)
    y1 = run_levels([("quad", 2 * k) for k in range(5)], padded(x), cos1, sin1, [wq])

    z = y1.reshape(2, 2, 2, 2, 2, 2, 2, 2, 2, 2, 2, LANE)[..., :P_SIZE]
    z = z.transpose(4, 6, 8, 1, 3, 5, 7, 9, 0, 2, 10, 11).reshape(8, 32, 2, 2, 2, P_SIZE)
    z = exchange(z)
    z = z.reshape(2, 2, 2, 2, 2, 2, 2, 2, 2, 2, 2, P_SIZE)
    z = z.transpose(8, 9, 3, 4, 0, 5, 1, 6, 2, 7, 10, 11).reshape(1024, 2, P_SIZE)
    lo_a = bits_of(place_x, 3)
    lo_b = place_y
    r = [(rows >> k) & 1 for k in range(10)]
    a2 = lo_a[0] + 2 * lo_a[1] + 4 * lo_a[2] + 8 * r[8] + 16 * r[9] + 32 * r[1] + 64 * r[3] + 128 * r[5]
    b2 = lo_b + 32 * (r[0] + 2 * r[2] + 4 * r[4] + 8 * r[6] + 16 * r[7])
    cos2, sin2 = tables(slope, a2, b2)
    levels2 = [("quad", 0), ("quad", 2), ("quad", 4), ("pair", 6), ("pair", 7)]
    y2 = run_levels(levels2, padded(z), cos2, sin2, [wq, wp])

    w = y2.reshape(2, 2, 2, 2, 2, 2, 2, 2, 2, 2, 2, LANE)[..., :P_SIZE]
    w = w.transpose(4, 6, 8, 2, 3, 5, 7, 9, 0, 1, 10, 11).reshape(8, 32, 2, 2, 2, P_SIZE)
    w = exchange(w)
    w = w.reshape(2, 2, 2, 2, 2, 2, 2, 2, 2, 2, 2, P_SIZE)
    w = w.transpose(10, 11, 8, 9, 0, 1, 2, 3, 4, 5, 6, 7)
    return w.reshape(2 * P_SIZE, 1, 1, 1024)


def solution(mesh):
    in_specs = (P(None, "gx", "gy", None), P(), P(), P())
    out_specs = P(None, "gx", "gy", None)
    return jax.shard_map(local, mesh=mesh, in_specs=in_specs, out_specs=out_specs, check_vma=False)
```

```python
import functools

import jax
import jax.numpy as jnp
from jax import lax
from jax.experimental import pallas as pl
from jax.experimental.pallas import tpu as pltpu
from jax.sharding import PartitionSpec as P

P_SIZE = 144
SIDE = 32
LANE = 256
WIDE = 384
F = 2 * P_SIZE


def padded(x):
    x = x.reshape(x.shape[:-2] + (F,))
    pad = [(0, 0)] * (x.ndim - 1) + [(0, WIDE - F)]
    return jnp.pad(x, pad)


def build_weights(wt_ref, m_ref):
    count = wt_ref.shape[0]
    zeros = jnp.zeros((P_SIZE, 128), jnp.float32)

    def ext(v):
        return jnp.concatenate([v, zeros], 1)

    for t in range(count):
        wt_ref[t, F:WIDE, :] = jnp.zeros((WIDE - F, wt_ref.shape[2]), wt_ref.dtype)
        for c in range(count):
            real = ext(m_ref[t, c, 0].astype(jnp.float32))
            imag = ext(m_ref[t, c, 1].astype(jnp.float32))
            top = real + pltpu.roll(-imag, P_SIZE, 1)
            bottom = imag + pltpu.roll(real, P_SIZE, 1)
            base = c * WIDE
            wt_ref[t, 0:P_SIZE, base:base + WIDE] = top.astype(wt_ref.dtype)
            wt_ref[t, P_SIZE:F, base:base + WIDE] = bottom.astype(wt_ref.dtype)


def class_pieces(c, run, period, rows):
    if run >= 8:
        return [pl.ds(g * period + c * run, run) for g in range(rows // period)]
    return [pl.ds(c * run + k, rows // period, stride=period) for k in range(run)]


def load_class(ref, c, run, period):
    chunks, rows = ref.shape[:2]
    pieces = []
    for s in class_pieces(c, run, period, rows):
        parts = [ref[q, s, :] for q in range(chunks)]
        pieces.append(jnp.concatenate(parts, 1))
    return pieces[0] if len(pieces) == 1 else jnp.concatenate(pieces, 0)


def store_class(ref, c, run, period, value):
    chunks, rows = ref.shape[:2]
    at = 0
    for s in class_pieces(c, run, period, rows):
        size = s.size
        for q in range(chunks):
            ref[q, s, :] = value[at:at + size, q * 128:(q + 1) * 128]
        at += size


def levels_kernel(levels, x_ref, cos_ref, sin_ref, *refs):
    count_w = (len(refs) - 3) // 2
    m_refs = refs[:count_w]
    o_ref, s0, s1 = refs[count_w:count_w + 3]
    w_refs = refs[count_w + 3:]
    for w_ref, m_ref in zip(w_refs, m_refs):
        build_weights(w_ref, m_ref)
    for q in range(WIDE // 128):
        s0[q] = x_ref[:, q * 128:(q + 1) * 128].astype(jnp.float32)
    bufs = (s0, s1)
    for index, (kind, pos) in enumerate(levels):
        src = bufs[index % 2]
        dst = bufs[(index + 1) % 2]
        count = 4 if kind == "quad" else 2
        run = 1 << pos
        period = run * count
        w_ref = w_refs[0] if kind == "quad" else w_refs[-1]
        children = [load_class(src, c, run, period).astype(jnp.bfloat16) for c in range(count)]
        stacked = jnp.concatenate(children, 1)
        for t in range(count):
            y = lax.dot_general(
                stacked, w_ref[t], (((1,), (1,)), ((), ())), preferred_element_type=jnp.float32
            )
            lane = lax.broadcasted_iota(jnp.int32, y.shape, 1)
            swapped = jnp.where(lane < P_SIZE, pltpu.roll(y, WIDE - P_SIZE, 1), pltpu.roll(y, P_SIZE, 1))
            cs = load_class(cos_ref, t, run, period)
            sn = load_class(sin_ref, t, run, period)
            out = (y * cs + swapped * sn).astype(jnp.bfloat16).astype(jnp.float32)
            store_class(dst, t, run, period, out)
    last = bufs[len(levels) % 2]
    for q in range(WIDE // 128):
        o_ref[:, q * 128:(q + 1) * 128] = last[q].astype(o_ref.dtype)


def run_levels(levels, x, cos_t, sin_t, m_list):
    rows = x.shape[0]
    vmem = pl.BlockSpec(memory_space=pltpu.VMEM)
    w_scratch = [
        pltpu.VMEM((m.shape[0], WIDE, m.shape[1] * WIDE), jnp.bfloat16) for m in m_list
    ]
    m_list = [jnp.pad(m, [(0, 0)] * 4 + [(0, LANE - P_SIZE)]) for m in m_list]
    return pl.pallas_call(
        functools.partial(levels_kernel, levels),
        out_shape=jax.ShapeDtypeStruct((rows, WIDE), jnp.bfloat16),
        in_specs=[vmem] * (3 + len(m_list)),
        out_specs=vmem,
        scratch_shapes=[pltpu.VMEM((WIDE // 128, rows, 128), jnp.float32)] * 2 + w_scratch,
        compiler_params=pltpu.CompilerParams(vmem_limit_bytes=60 * 1024 * 1024),
    )(x, cos_t, sin_t, *m_list)


def bits_of(value, count):
    return [(value >> k) & 1 for k in range(count)]


def tables(slope, a, b):
    center_x = (a.astype(jnp.float32) + 0.5) / 256.0 - 0.5
    center_y = (b.astype(jnp.float32) + 0.5) / 1024.0 - 0.5
    angle = slope[0][None, :] * center_x[:, None] + slope[1][None, :] * center_y[:, None]
    cosine = jnp.cos(angle)
    sine = jnp.sin(angle)
    pad = [(0, 0), (0, WIDE - F)]

    def chunked(v):
        return jnp.pad(v, pad).reshape(-1, WIDE // 128, 128).transpose(1, 0, 2)

    return chunked(jnp.concatenate([cosine, cosine], 1)), chunked(jnp.concatenate([-sine, sine], 1))


def exchange(z):
    shape = z.shape
    z = z.reshape((shape[0] * shape[1],) + shape[2:])
    z = lax.all_to_all(z, ("gx", "gy"), 0, 0, tiled=True)
    return z.reshape(shape)


def local(source, slope, quad, pair):
    place_x = lax.axis_index("gx")
    place_y = lax.axis_index("gy")
    wq = quad.reshape(4, 4, 2, P_SIZE, P_SIZE)
    wp = pair.reshape(2, 2, 2, P_SIZE, P_SIZE)
    rows = jnp.arange(1024, dtype=jnp.int32)

    i1 = sum(((rows >> (2 * k + 1)) & 1) << k for k in range(5))
    j1 = sum(((rows >> (2 * k)) & 1) << k for k in range(5))
    cos1, sin1 = tables(slope, place_x * 32 + i1, place_y * 32 + j1)
    x = source.reshape(2, P_SIZE, 2, 2, 2, 2, 2, 2, 2, 2, 2, 2)
    x = x.transpose(2, 7, 3, 8, 4, 9, 5, 10, 6, 11, 0, 1).reshape(1024, 2, P_SIZE)
    y1 = run_levels([("quad", 2 * k) for k in range(5)], padded(x), cos1, sin1, [wq])

    z = y1[:, :F].reshape(2, 2, 2, 2, 2, 2, 2, 2, 2, 2, 2, P_SIZE)
    z = z.transpose(4, 6, 8, 1, 3, 5, 7, 9, 0, 2, 10, 11).reshape(8, 32, 2, 2, 2, P_SIZE)
    z = exchange(z)
    z = z.reshape(2, 2, 2, 2, 2, 2, 2, 2, 2, 2, 2, P_SIZE)
    z = z.transpose(8, 9, 3, 4, 0, 5, 1, 6, 2, 7, 10, 11).reshape(1024, 2, P_SIZE)
    lo_a = bits_of(place_x, 3)
    lo_b = place_y
    r = [(rows >> k) & 1 for k in range(10)]
    a2 = lo_a[0] + 2 * lo_a[1] + 4 * lo_a[2] + 8 * r[8] + 16 * r[9] + 32 * r[1] + 64 * r[3] + 128 * r[5]
    b2 = lo_b + 32 * (r[0] + 2 * r[2] + 4 * r[4] + 8 * r[6] + 16 * r[7])
    cos2, sin2 = tables(slope, a2, b2)
    levels2 = [("quad", 0), ("quad", 2), ("quad", 4), ("pair", 6), ("pair", 7)]
    y2 = run_levels(levels2, padded(z), cos2, sin2, [wq, wp])

    w = y2[:, :F].reshape(2, 2, 2, 2, 2, 2, 2, 2, 2, 2, 2, P_SIZE)
    w = w.transpose(4, 6, 8, 2, 3, 5, 7, 9, 0, 1, 10, 11).reshape(8, 32, 2, 2, 2, P_SIZE)
    w = exchange(w)
    w = w.reshape(2, 2, 2, 2, 2, 2, 2, 2, 2, 2, 2, P_SIZE)
    w = w.transpose(10, 11, 8, 9, 0, 1, 2, 3, 4, 5, 6, 7)
    return w.reshape(2 * P_SIZE, 1, 1, 1024)


def solution(mesh):
    in_specs = (P(None, "gx", "gy", None), P(), P(), P())
    out_specs = P(None, "gx", "gy", None)
    return jax.shard_map(local, mesh=mesh, in_specs=in_specs, out_specs=out_specs, check_vma=False)
```

```python
import functools

import jax
import jax.numpy as jnp
from jax import lax
from jax.experimental import pallas as pl
from jax.experimental.pallas import tpu as pltpu
from jax.sharding import PartitionSpec as P

P_SIZE = 144
SIDE = 32
LANE = 256
WIDE = 384
F = 2 * P_SIZE


def padded(x):
    x = x.reshape(x.shape[:-2] + (F,))
    pad = [(0, 0)] * (x.ndim - 1) + [(0, WIDE - F)]
    return jnp.pad(x, pad)


def build_weights(wt_ref, m_ref):
    count = wt_ref.shape[0]
    zeros = jnp.zeros((P_SIZE, 128), jnp.float32)

    def ext(v):
        return jnp.concatenate([v, zeros], 1)

    for t in range(count):
        wt_ref[t, F:WIDE, :] = jnp.zeros((WIDE - F, wt_ref.shape[2]), wt_ref.dtype)
        for c in range(count):
            real = ext(m_ref[t, c, 0].astype(jnp.float32))
            imag = ext(m_ref[t, c, 1].astype(jnp.float32))
            top = real + pltpu.roll(-imag, P_SIZE, 1)
            bottom = imag + pltpu.roll(real, P_SIZE, 1)
            base = c * WIDE
            wt_ref[t, 0:P_SIZE, base:base + WIDE] = top.astype(wt_ref.dtype)
            wt_ref[t, P_SIZE:F, base:base + WIDE] = bottom.astype(wt_ref.dtype)


def class_pieces(c, run, period, rows):
    if run >= 8:
        return [pl.ds(g * period + c * run, run) for g in range(rows // period)]
    return [pl.ds(c * run + k, rows // period, stride=period) for k in range(run)]


def load_class(ref, c, run, period):
    chunks, rows = ref.shape[:2]
    pieces = []
    for s in class_pieces(c, run, period, rows):
        parts = [ref[q, s, :] for q in range(chunks)]
        pieces.append(jnp.concatenate(parts, 1))
    return pieces[0] if len(pieces) == 1 else jnp.concatenate(pieces, 0)


def store_class(ref, c, run, period, value):
    chunks, rows = ref.shape[:2]
    at = 0
    for s in class_pieces(c, run, period, rows):
        size = s.size
        for q in range(chunks):
            ref[q, s, :] = value[at:at + size, q * 128:(q + 1) * 128]
        at += size


def levels_kernel(levels, x_ref, cos_ref, sin_ref, *refs):
    count_w = (len(refs) - 3) // 2
    m_refs = refs[:count_w]
    o_ref, s0, s1 = refs[count_w:count_w + 3]
    w_refs = refs[count_w + 3:]
    for w_ref, m_ref in zip(w_refs, m_refs):
        build_weights(w_ref, m_ref)
    for q in range(WIDE // 128):
        s0[q] = x_ref[:, q * 128:(q + 1) * 128].astype(jnp.float32)
    bufs = (s0, s1)
    for index, (kind, pos) in enumerate(levels):
        src = bufs[index % 2]
        dst = bufs[(index + 1) % 2]
        count = 4 if kind == "quad" else 2
        run = 1 << pos
        period = run * count
        w_ref = w_refs[0] if kind == "quad" else w_refs[-1]
        children = [load_class(src, c, run, period).astype(jnp.bfloat16) for c in range(count)]
        stacked = jnp.concatenate(children, 1)
        for t in range(count):
            y = lax.dot_general(
                stacked, w_ref[t], (((1,), (1,)), ((), ())), preferred_element_type=jnp.float32
            )
            lane = lax.broadcasted_iota(jnp.int32, y.shape, 1)
            swapped = jnp.where(lane < P_SIZE, pltpu.roll(y, WIDE - P_SIZE, 1), pltpu.roll(y, P_SIZE, 1))
            cs = load_class(cos_ref, t, run, period)
            sn = load_class(sin_ref, t, run, period)
            out = (y * cs + swapped * sn).astype(jnp.bfloat16).astype(jnp.float32)
            store_class(dst, t, run, period, out)
    last = bufs[len(levels) % 2]
    for q in range(WIDE // 128):
        o_ref[:, q * 128:(q + 1) * 128] = last[q].astype(o_ref.dtype)


def run_levels(levels, x, cos_t, sin_t, m_list):
    rows = x.shape[0]
    vmem = pl.BlockSpec(memory_space=pltpu.VMEM)
    w_scratch = [
        pltpu.VMEM((m.shape[0], WIDE, m.shape[1] * WIDE), jnp.bfloat16) for m in m_list
    ]
    m_list = [jnp.pad(m, [(0, 0)] * 4 + [(0, LANE - P_SIZE)]) for m in m_list]
    return pl.pallas_call(
        functools.partial(levels_kernel, levels),
        out_shape=jax.ShapeDtypeStruct((rows, WIDE), jnp.bfloat16),
        in_specs=[vmem] * (3 + len(m_list)),
        out_specs=vmem,
        scratch_shapes=[pltpu.VMEM((WIDE // 128, rows, 128), jnp.float32)] * 2 + w_scratch,
        compiler_params=pltpu.CompilerParams(vmem_limit_bytes=60 * 1024 * 1024),
    )(x, cos_t, sin_t, *m_list)


def bits_of(value, count):
    return [(value >> k) & 1 for k in range(count)]


def tables(slope, a, b):
    center_x = (a.astype(jnp.float32) + 0.5) / 256.0 - 0.5
    center_y = (b.astype(jnp.float32) + 0.5) / 1024.0 - 0.5
    angle = slope[0][None, :] * center_x[:, None] + slope[1][None, :] * center_y[:, None]
    cosine = jnp.cos(angle)
    sine = jnp.sin(angle)
    pad = [(0, 0), (0, WIDE - F)]

    def chunked(v):
        return jnp.pad(v, pad).reshape(-1, WIDE // 128, 128).transpose(1, 0, 2)

    return chunked(jnp.concatenate([cosine, cosine], 1)), chunked(jnp.concatenate([-sine, sine], 1))


def exchange(z):
    shape = z.shape
    z = z.reshape(shape[0] * shape[1], 1, -1)
    z = lax.all_to_all(z, ("gx", "gy"), 0, 0, tiled=True)
    return z.reshape(shape)


def local(source, slope, quad, pair):
    place_x = lax.axis_index("gx")
    place_y = lax.axis_index("gy")
    wq = quad.reshape(4, 4, 2, P_SIZE, P_SIZE)
    wp = pair.reshape(2, 2, 2, P_SIZE, P_SIZE)
    rows = jnp.arange(1024, dtype=jnp.int32)

    i1 = sum(((rows >> (2 * k + 1)) & 1) << k for k in range(5))
    j1 = sum(((rows >> (2 * k)) & 1) << k for k in range(5))
    cos1, sin1 = tables(slope, place_x * 32 + i1, place_y * 32 + j1)
    x = source.reshape(2, P_SIZE, 2, 2, 2, 2, 2, 2, 2, 2, 2, 2)
    x = x.transpose(2, 7, 3, 8, 4, 9, 5, 10, 6, 11, 0, 1).reshape(1024, 2, P_SIZE)
    y1 = run_levels([("quad", 2 * k) for k in range(5)], padded(x), cos1, sin1, [wq])

    z = y1[:, :F].reshape(2, 2, 2, 2, 2, 2, 2, 2, 2, 2, 2, P_SIZE)
    z = z.transpose(4, 6, 8, 1, 3, 5, 7, 9, 0, 2, 10, 11).reshape(8, 32, 2, 2, 2, P_SIZE)
    z = exchange(z)
    z = z.reshape(2, 2, 2, 2, 2, 2, 2, 2, 2, 2, 2, P_SIZE)
    z = z.transpose(8, 9, 3, 4, 0, 5, 1, 6, 2, 7, 10, 11).reshape(1024, 2, P_SIZE)
    lo_a = bits_of(place_x, 3)
    lo_b = place_y
    r = [(rows >> k) & 1 for k in range(10)]
    a2 = lo_a[0] + 2 * lo_a[1] + 4 * lo_a[2] + 8 * r[8] + 16 * r[9] + 32 * r[1] + 64 * r[3] + 128 * r[5]
    b2 = lo_b + 32 * (r[0] + 2 * r[2] + 4 * r[4] + 8 * r[6] + 16 * r[7])
    cos2, sin2 = tables(slope, a2, b2)
    levels2 = [("quad", 0), ("quad", 2), ("quad", 4), ("pair", 6), ("pair", 7)]
    y2 = run_levels(levels2, padded(z), cos2, sin2, [wq, wp])

    w = y2[:, :F].reshape(2, 2, 2, 2, 2, 2, 2, 2, 2, 2, 2, P_SIZE)
    w = w.transpose(4, 6, 8, 2, 3, 5, 7, 9, 0, 1, 10, 11).reshape(8, 32, 2, 2, 2, P_SIZE)
    w = exchange(w)
    w = w.reshape(2, 2, 2, 2, 2, 2, 2, 2, 2, 2, 2, P_SIZE)
    w = w.transpose(10, 11, 8, 9, 0, 1, 2, 3, 4, 5, 6, 7)
    return w.reshape(2 * P_SIZE, 1, 1, 1024)


def solution(mesh):
    in_specs = (P(None, "gx", "gy", None), P(), P(), P())
    out_specs = P(None, "gx", "gy", None)
    return jax.shard_map(local, mesh=mesh, in_specs=in_specs, out_specs=out_specs, check_vma=False)
```

```python
import functools

import jax
import jax.numpy as jnp
from jax import lax
from jax.experimental import pallas as pl
from jax.experimental.pallas import tpu as pltpu
from jax.sharding import PartitionSpec as P

P_SIZE = 144
SIDE = 32
LANE = 256
WIDE = 384
F = 2 * P_SIZE


def padded(x):
    x = x.reshape(x.shape[:-2] + (F,))
    pad = [(0, 0)] * (x.ndim - 1) + [(0, WIDE - F)]
    return jnp.pad(x, pad)


def build_weights(wt_ref, m_ref):
    count = wt_ref.shape[0]
    zeros = jnp.zeros((P_SIZE, 128), jnp.float32)

    def ext(v):
        return jnp.concatenate([v, zeros], 1)

    for t in range(count):
        wt_ref[t, F:WIDE, :] = jnp.zeros((WIDE - F, wt_ref.shape[2]), wt_ref.dtype)
        for c in range(count):
            real = ext(m_ref[t, c, 0].astype(jnp.float32))
            imag = ext(m_ref[t, c, 1].astype(jnp.float32))
            top = real + pltpu.roll(-imag, P_SIZE, 1)
            bottom = imag + pltpu.roll(real, P_SIZE, 1)
            base = c * WIDE
            wt_ref[t, 0:P_SIZE, base:base + WIDE] = top.astype(wt_ref.dtype)
            wt_ref[t, P_SIZE:F, base:base + WIDE] = bottom.astype(wt_ref.dtype)


def class_pieces(fixed, rows):
    low = min(fixed)
    base = sum(v << p for p, v in fixed.items())
    free = [p for p in range(rows.bit_length() - 1) if p not in fixed]
    if (1 << low) >= 8:
        outer = [p for p in free if p > low]
        starts = []
        for k in range(1 << len(outer)):
            starts.append(base + sum(((k >> i) & 1) << p for i, p in enumerate(outer)))
        return [pl.ds(st, 1 << low) for st in starts]
    above = [p for p in fixed if p > low]
    top = min(above) if above else rows.bit_length() - 1
    inner = [p for p in free if low < p < top]
    outer = [p for p in free if p < low or p > top]
    slices = []
    for k in range(1 << len(outer)):
        st = base + sum(((k >> i) & 1) << p for i, p in enumerate(outer))
        slices.append(pl.ds(st, 1 << len(inner), stride=1 << (low + 1)))
    return slices


def load_class(ref, fixed):
    chunks, rows = ref.shape[:2]
    pieces = []
    for s in class_pieces(fixed, rows):
        parts = [ref[q, s, :] for q in range(chunks)]
        pieces.append(jnp.concatenate(parts, 1))
    return pieces[0] if len(pieces) == 1 else jnp.concatenate(pieces, 0)


def store_class(ref, fixed, value):
    chunks, rows = ref.shape[:2]
    at = 0
    for s in class_pieces(fixed, rows):
        size = s.size
        for q in range(chunks):
            ref[q, s, :] = value[at:at + size, q * 128:(q + 1) * 128]
        at += size


def class_bits(bits, c):
    if len(bits) == 2:
        return {bits[0]: c >> 1, bits[1]: c & 1}
    return {bits[0]: c}


def levels_kernel(levels, packed_in, x_ref, cos_ref, sin_ref, *refs):
    count_w = (len(refs) - 3) // 2
    m_refs = refs[:count_w]
    o_ref, s0, s1 = refs[count_w:count_w + 3]
    w_refs = refs[count_w + 3:]
    for w_ref, m_ref in zip(w_refs, m_refs):
        build_weights(w_ref, m_ref)
    rows = s0.shape[1]
    block = rows // 4
    if packed_in:
        whole = x_ref[...].astype(jnp.float32)
        lane = lax.broadcasted_iota(jnp.int32, (block, WIDE), 1)
        for b in range(4):
            piece = whole if b == 0 else pltpu.roll(whole, 4 * F - b * F, 1)
            piece = jnp.where(lane < F, piece[:, :WIDE], 0.0)
            for q in range(WIDE // 128):
                s0[q, b * block:(b + 1) * block, :] = piece[:, q * 128:(q + 1) * 128]
    else:
        for q in range(WIDE // 128):
            s0[q] = x_ref[:, q * 128:(q + 1) * 128].astype(jnp.float32)
    bufs = (s0, s1)
    for index, (kind, bits) in enumerate(levels):
        src = bufs[index % 2]
        dst = bufs[(index + 1) % 2]
        count = 4 if kind == "quad" else 2
        w_ref = w_refs[0] if kind == "quad" else w_refs[-1]
        children = [load_class(src, class_bits(bits, c)).astype(jnp.bfloat16) for c in range(count)]
        stacked = jnp.concatenate(children, 1)
        for t in range(count):
            fixed = class_bits(bits, t)
            y = lax.dot_general(
                stacked, w_ref[t], (((1,), (1,)), ((), ())), preferred_element_type=jnp.float32
            )
            lane = lax.broadcasted_iota(jnp.int32, y.shape, 1)
            swapped = jnp.where(lane < P_SIZE, pltpu.roll(y, WIDE - P_SIZE, 1), pltpu.roll(y, P_SIZE, 1))
            cs = load_class(cos_ref, fixed)
            sn = load_class(sin_ref, fixed)
            out = (y * cs + swapped * sn).astype(jnp.bfloat16).astype(jnp.float32)
            store_class(dst, fixed, out)
    last = bufs[len(levels) % 2]
    total = None
    pad = jnp.zeros((block, 4 * F - WIDE), jnp.float32)
    for b in range(4):
        piece = jnp.concatenate([last[q, b * block:(b + 1) * block, :] for q in range(WIDE // 128)], 1)
        piece = jnp.concatenate([piece, pad], 1)
        if b:
            piece = pltpu.roll(piece, b * F, 1)
        total = piece if total is None else total + piece
    o_ref[...] = total.astype(o_ref.dtype)


def run_levels(levels, packed_in, x, cos_t, sin_t, m_list):
    rows = 1024
    vmem = pl.BlockSpec(memory_space=pltpu.VMEM)
    w_scratch = [
        pltpu.VMEM((m.shape[0], WIDE, m.shape[1] * WIDE), jnp.bfloat16) for m in m_list
    ]
    m_list = [jnp.pad(m, [(0, 0)] * 4 + [(0, LANE - P_SIZE)]) for m in m_list]
    return pl.pallas_call(
        functools.partial(levels_kernel, levels, packed_in),
        out_shape=jax.ShapeDtypeStruct((rows // 4, 4 * F), jnp.bfloat16),
        in_specs=[vmem] * (3 + len(m_list)),
        out_specs=vmem,
        scratch_shapes=[pltpu.VMEM((WIDE // 128, rows, 128), jnp.float32)] * 2 + w_scratch,
        compiler_params=pltpu.CompilerParams(vmem_limit_bytes=60 * 1024 * 1024),
    )(x, cos_t, sin_t, *m_list)


def bits_of(value, count):
    return [(value >> k) & 1 for k in range(count)]


def tables(slope, a, b):
    center_x = (a.astype(jnp.float32) + 0.5) / 256.0 - 0.5
    center_y = (b.astype(jnp.float32) + 0.5) / 1024.0 - 0.5
    angle = slope[0][None, :] * center_x[:, None] + slope[1][None, :] * center_y[:, None]
    cosine = jnp.cos(angle)
    sine = jnp.sin(angle)
    pad = [(0, 0), (0, WIDE - F)]

    def chunked(v):
        return jnp.pad(v, pad).reshape(-1, WIDE // 128, 128).transpose(1, 0, 2)

    return chunked(jnp.concatenate([cosine, cosine], 1)), chunked(jnp.concatenate([-sine, sine], 1))


def exchange(z):
    shape = z.shape
    z = z.transpose(0, 1, 4, 2, 3, 5).reshape(shape[0] * shape[1], 2, -1)
    z = lax.all_to_all(z, ("gx", "gy"), 0, 0, tiled=True)
    z = z.reshape(shape[0], shape[1], 2, 2, 2, shape[5])
    return z.transpose(0, 1, 3, 4, 2, 5)


def local(source, slope, quad, pair):
    place_x = lax.axis_index("gx")
    place_y = lax.axis_index("gy")
    wq = quad.reshape(4, 4, 2, P_SIZE, P_SIZE)
    wp = pair.reshape(2, 2, 2, P_SIZE, P_SIZE)
    rows = jnp.arange(1024, dtype=jnp.int32)

    cos1, sin1 = tables(slope, place_x * 32 + (rows >> 5), place_y * 32 + (rows & 31))
    x = source.reshape(F, 1024).T
    x = jnp.pad(x, [(0, 0), (0, WIDE - F)])
    levels1 = [("quad", (k + 5, k)) for k in range(5)]
    y1 = run_levels(levels1, False, x, cos1, sin1, [wq])
    z = lax.all_to_all(y1, ("gx", "gy"), 0, 0, tiled=True)
    lo_a = place_x & 1
    lo_a = lo_a + 2 * ((place_x >> 1) & 1) + 4 * ((place_x >> 2) & 1)
    a2 = lo_a + 8 * ((rows >> 8) & 1) + 16 * ((rows >> 9) & 1) + 32 * ((rows >> 5) & 7)
    b2 = place_y + 32 * (rows & 31)
    cos2, sin2 = tables(slope, a2, b2)
    levels2 = [("quad", (5, 0)), ("quad", (6, 1)), ("quad", (7, 2)), ("pair", (3,)), ("pair", (4,))]
    y2 = run_levels(levels2, True, z, cos2, sin2, [wq, wp])
    w = lax.all_to_all(y2, ("gx", "gy"), 0, 0, tiled=True)
    w = w.reshape(256, 4, F).transpose(2, 1, 0)
    return w.reshape(F, 1, 1, 1024)


def solution(mesh):
    in_specs = (P(None, "gx", "gy", None), P(), P(), P())
    out_specs = P(None, "gx", "gy", None)
    return jax.shard_map(local, mesh=mesh, in_specs=in_specs, out_specs=out_specs, check_vma=False)
```

```python
import functools

import jax
import jax.numpy as jnp
from jax import lax
from jax.experimental import pallas as pl
from jax.experimental.pallas import tpu as pltpu
from jax.sharding import PartitionSpec as P

P_SIZE = 144
SIDE = 32
LANE = 256
WIDE = 384
F = 2 * P_SIZE


def padded(x):
    x = x.reshape(x.shape[:-2] + (F,))
    pad = [(0, 0)] * (x.ndim - 1) + [(0, WIDE - F)]
    return jnp.pad(x, pad)


def build_weights(wt_ref, m_ref):
    count = wt_ref.shape[0]
    zeros = jnp.zeros((P_SIZE, 128), jnp.float32)

    def ext(v):
        return jnp.concatenate([v, zeros], 1)

    for t in range(count):
        wt_ref[t, F:WIDE, :] = jnp.zeros((WIDE - F, wt_ref.shape[2]), wt_ref.dtype)
        for c in range(count):
            real = ext(m_ref[t, c, 0].astype(jnp.float32))
            imag = ext(m_ref[t, c, 1].astype(jnp.float32))
            top = real + pltpu.roll(-imag, P_SIZE, 1)
            bottom = imag + pltpu.roll(real, P_SIZE, 1)
            base = c * WIDE
            wt_ref[t, 0:P_SIZE, base:base + WIDE] = top.astype(wt_ref.dtype)
            wt_ref[t, P_SIZE:F, base:base + WIDE] = bottom.astype(wt_ref.dtype)


def class_pieces(fixed, rows):
    low = min(fixed)
    base = sum(v << p for p, v in fixed.items())
    free = [p for p in range(rows.bit_length() - 1) if p not in fixed]
    if (1 << low) >= 8:
        outer = [p for p in free if p > low]
        starts = []
        for k in range(1 << len(outer)):
            starts.append(base + sum(((k >> i) & 1) << p for i, p in enumerate(outer)))
        return [pl.ds(st, 1 << low) for st in starts]
    above = [p for p in fixed if p > low]
    top = min(above) if above else rows.bit_length() - 1
    inner = [p for p in free if low < p < top]
    outer = [p for p in free if p < low or p > top]
    slices = []
    for k in range(1 << len(outer)):
        st = base + sum(((k >> i) & 1) << p for i, p in enumerate(outer))
        slices.append(pl.ds(st, 1 << len(inner), stride=1 << (low + 1)))
    return slices


def load_class(ref, fixed):
    chunks, rows = ref.shape[:2]
    pieces = []
    for s in class_pieces(fixed, rows):
        parts = [ref[q, s, :] for q in range(chunks)]
        pieces.append(jnp.concatenate(parts, 1))
    return pieces[0] if len(pieces) == 1 else jnp.concatenate(pieces, 0)


def store_class(ref, fixed, value):
    chunks, rows = ref.shape[:2]
    at = 0
    for s in class_pieces(fixed, rows):
        size = s.size
        for q in range(chunks):
            ref[q, s, :] = value[at:at + size, q * 128:(q + 1) * 128]
        at += size


def class_bits(bits, c):
    if len(bits) == 2:
        return {bits[0]: c >> 1, bits[1]: c & 1}
    return {bits[0]: c}


def levels_kernel(levels, packed_in, x_ref, f_ref, *refs):
    count_w = (len(refs) - 5) // 2
    m_refs = refs[:count_w]
    o_ref, s0, s1, cos_ref, sin_ref = refs[count_w:count_w + 5]
    w_refs = refs[count_w + 5:]
    build_tables(cos_ref, sin_ref, f_ref)
    for w_ref, m_ref in zip(w_refs, m_refs):
        build_weights(w_ref, m_ref)
    rows = s0.shape[1]
    block = rows // 4
    if packed_in:
        whole = x_ref[...].astype(jnp.float32)
        lane = lax.broadcasted_iota(jnp.int32, (block, WIDE), 1)
        for b in range(4):
            piece = whole if b == 0 else pltpu.roll(whole, 4 * F - b * F, 1)
            piece = jnp.where(lane < F, piece[:, :WIDE], 0.0)
            for q in range(WIDE // 128):
                s0[q, b * block:(b + 1) * block, :] = piece[:, q * 128:(q + 1) * 128]
    else:
        for q in range(WIDE // 128):
            s0[q] = x_ref[:, q * 128:(q + 1) * 128].astype(jnp.float32)
    bufs = (s0, s1)
    for index, (kind, bits) in enumerate(levels):
        src = bufs[index % 2]
        dst = bufs[(index + 1) % 2]
        count = 4 if kind == "quad" else 2
        w_ref = w_refs[0] if kind == "quad" else w_refs[-1]
        children = [load_class(src, class_bits(bits, c)).astype(jnp.bfloat16) for c in range(count)]
        stacked = jnp.concatenate(children, 1)
        for t in range(count):
            fixed = class_bits(bits, t)
            y = lax.dot_general(
                stacked, w_ref[t], (((1,), (1,)), ((), ())), preferred_element_type=jnp.float32
            )
            lane = lax.broadcasted_iota(jnp.int32, y.shape, 1)
            swapped = jnp.where(lane < P_SIZE, pltpu.roll(y, WIDE - P_SIZE, 1), pltpu.roll(y, P_SIZE, 1))
            cs = load_class(cos_ref, fixed)
            sn = load_class(sin_ref, fixed)
            out = (y * cs + swapped * sn).astype(jnp.bfloat16).astype(jnp.float32)
            store_class(dst, fixed, out)
    last = bufs[len(levels) % 2]
    total = None
    pad = jnp.zeros((block, 4 * F - WIDE), jnp.float32)
    for b in range(4):
        piece = jnp.concatenate([last[q, b * block:(b + 1) * block, :] for q in range(WIDE // 128)], 1)
        piece = jnp.concatenate([piece, pad], 1)
        if b:
            piece = pltpu.roll(piece, b * F, 1)
        total = piece if total is None else total + piece
    o_ref[...] = total.astype(o_ref.dtype)


def run_levels(levels, packed_in, x, f_t, m_list):
    rows = 1024
    vmem = pl.BlockSpec(memory_space=pltpu.VMEM)
    w_scratch = [
        pltpu.VMEM((m.shape[0], WIDE, m.shape[1] * WIDE), jnp.bfloat16) for m in m_list
    ]
    m_list = [jnp.pad(m, [(0, 0)] * 4 + [(0, LANE - P_SIZE)]) for m in m_list]
    return pl.pallas_call(
        functools.partial(levels_kernel, levels, packed_in),
        out_shape=jax.ShapeDtypeStruct((rows // 4, 4 * F), jnp.bfloat16),
        in_specs=[vmem] * (2 + len(m_list)),
        out_specs=vmem,
        scratch_shapes=[pltpu.VMEM((WIDE // 128, rows, 128), jnp.float32)] * 4 + w_scratch,
        compiler_params=pltpu.CompilerParams(vmem_limit_bytes=60 * 1024 * 1024),
    )(x, f_t, *m_list)


def bits_of(value, count):
    return [(value >> k) & 1 for k in range(count)]


def factors(slope, a, b):
    center_x = (a.astype(jnp.float32) + 0.5) / 256.0 - 0.5
    center_y = (b.astype(jnp.float32) + 0.5) / 1024.0 - 0.5
    part_a = slope[0][None, :] * center_x[:, None]
    part_b = slope[1][None, :] * center_y[:, None]
    pad = [(0, 0), (0, WIDE - F)]

    def lanes(v):
        return jnp.pad(jnp.concatenate([v, v], 1), pad)

    return jnp.stack([lanes(jnp.cos(part_a)), lanes(jnp.sin(part_a)), lanes(jnp.cos(part_b)), lanes(jnp.sin(part_b))])


def build_tables(cos_ref, sin_ref, f_ref):
    groups = f_ref.shape[1]
    cb = f_ref[2]
    sb = f_ref[3]
    lane = lax.broadcasted_iota(jnp.int32, cb.shape, 1)
    for i in range(groups):
        ca = f_ref[0, i:i + 1, :]
        sa = f_ref[1, i:i + 1, :]
        cosine = ca * cb - sa * sb
        sine = sa * cb + ca * sb
        sine = jnp.where(lane < P_SIZE, -sine, sine)
        rows = pl.ds(i * groups, groups)
        for q in range(WIDE // 128):
            cos_ref[q, rows, :] = cosine[:, q * 128:(q + 1) * 128]
            sin_ref[q, rows, :] = sine[:, q * 128:(q + 1) * 128]


def exchange(z):
    shape = z.shape
    z = z.transpose(0, 1, 4, 2, 3, 5).reshape(shape[0] * shape[1], 2, -1)
    z = lax.all_to_all(z, ("gx", "gy"), 0, 0, tiled=True)
    z = z.reshape(shape[0], shape[1], 2, 2, 2, shape[5])
    return z.transpose(0, 1, 3, 4, 2, 5)


def local(source, slope, quad, pair):
    place_x = lax.axis_index("gx")
    place_y = lax.axis_index("gy")
    wq = quad.reshape(4, 4, 2, P_SIZE, P_SIZE)
    wp = pair.reshape(2, 2, 2, P_SIZE, P_SIZE)
    group = jnp.arange(32, dtype=jnp.int32)

    f1 = factors(slope, place_x * 32 + group, place_y * 32 + group)
    x = source.reshape(F, 1024).T
    x = jnp.pad(x, [(0, 0), (0, WIDE - F)])
    levels1 = [("quad", (k + 5, k)) for k in range(5)]
    y1 = run_levels(levels1, False, x, f1, [wq])
    z = lax.all_to_all(y1, ("gx", "gy"), 0, 0, tiled=True)
    a2 = place_x + 8 * ((group >> 3) & 1) + 16 * ((group >> 4) & 1) + 32 * (group & 7)
    b2 = place_y + 32 * group
    f2 = factors(slope, a2, b2)
    levels2 = [("quad", (5, 0)), ("quad", (6, 1)), ("quad", (7, 2)), ("pair", (3,)), ("pair", (4,))]
    y2 = run_levels(levels2, True, z, f2, [wq, wp])
    w = lax.all_to_all(y2, ("gx", "gy"), 0, 0, tiled=True)
    w = w.reshape(256, 4, F).transpose(2, 1, 0)
    return w.reshape(F, 1, 1, 1024)


def solution(mesh):
    in_specs = (P(None, "gx", "gy", None), P(), P(), P())
    out_specs = P(None, "gx", "gy", None)
    return jax.shard_map(local, mesh=mesh, in_specs=in_specs, out_specs=out_specs, check_vma=False)
```

```python
import functools

import jax
import jax.numpy as jnp
from jax import lax
from jax.experimental import pallas as pl
from jax.experimental.pallas import tpu as pltpu
from jax.sharding import PartitionSpec as P

P_SIZE = 144
SIDE = 32
LANE = 256
WIDE = 384
F = 2 * P_SIZE


def padded(x):
    x = x.reshape(x.shape[:-2] + (F,))
    pad = [(0, 0)] * (x.ndim - 1) + [(0, WIDE - F)]
    return jnp.pad(x, pad)


def build_weights(wt_ref, m_ref):
    count = wt_ref.shape[0]
    zeros = jnp.zeros((P_SIZE, 128), jnp.float32)

    def ext(v):
        return jnp.concatenate([v, zeros], 1)

    for t in range(count):
        wt_ref[t, F:WIDE, :] = jnp.zeros((WIDE - F, wt_ref.shape[2]), wt_ref.dtype)
        for c in range(count):
            real = ext(m_ref[t, c, 0].astype(jnp.float32))
            imag = ext(m_ref[t, c, 1].astype(jnp.float32))
            top = real + pltpu.roll(-imag, P_SIZE, 1)
            bottom = imag + pltpu.roll(real, P_SIZE, 1)
            base = c * WIDE
            wt_ref[t, 0:P_SIZE, base:base + WIDE] = top.astype(wt_ref.dtype)
            wt_ref[t, P_SIZE:F, base:base + WIDE] = bottom.astype(wt_ref.dtype)


def class_pieces(fixed, rows):
    low = min(fixed)
    base = sum(v << p for p, v in fixed.items())
    free = [p for p in range(rows.bit_length() - 1) if p not in fixed]
    if (1 << low) >= 8:
        outer = [p for p in free if p > low]
        starts = []
        for k in range(1 << len(outer)):
            starts.append(base + sum(((k >> i) & 1) << p for i, p in enumerate(outer)))
        return [pl.ds(st, 1 << low) for st in starts]
    above = [p for p in fixed if p > low]
    top = min(above) if above else rows.bit_length() - 1
    inner = [p for p in free if low < p < top]
    outer = [p for p in free if p < low or p > top]
    slices = []
    for k in range(1 << len(outer)):
        st = base + sum(((k >> i) & 1) << p for i, p in enumerate(outer))
        slices.append(pl.ds(st, 1 << len(inner), stride=1 << (low + 1)))
    return slices


def load_class(ref, fixed):
    chunks, rows = ref.shape[:2]
    pieces = []
    for s in class_pieces(fixed, rows):
        parts = [ref[q, s, :] for q in range(chunks)]
        pieces.append(jnp.concatenate(parts, 1))
    return pieces[0] if len(pieces) == 1 else jnp.concatenate(pieces, 0)


def store_class(ref, fixed, value):
    chunks, rows = ref.shape[:2]
    at = 0
    for s in class_pieces(fixed, rows):
        size = s.size
        for q in range(chunks):
            ref[q, s, :] = value[at:at + size, q * 128:(q + 1) * 128]
        at += size


def class_bits(bits, c):
    if len(bits) == 2:
        return {bits[0]: c >> 1, bits[1]: c & 1}
    return {bits[0]: c}


def levels_kernel(levels, packed_in, x_ref, f_ref, *refs):
    count_w = (len(refs) - 5) // 2
    m_refs = refs[:count_w]
    o_ref, s0, s1, cos_ref, sin_ref = refs[count_w:count_w + 5]
    w_refs = refs[count_w + 5:]
    build_tables(cos_ref, sin_ref, f_ref)
    for w_ref, m_ref in zip(w_refs, m_refs):
        build_weights(w_ref, m_ref)
    rows = s0.shape[1]
    block = rows // 4
    if packed_in:
        whole = x_ref[...].astype(jnp.float32)
        lane = lax.broadcasted_iota(jnp.int32, (block, WIDE), 1)
        for b in range(4):
            piece = whole if b == 0 else pltpu.roll(whole, 4 * F - b * F, 1)
            piece = jnp.where(lane < F, piece[:, :WIDE], 0.0)
            for q in range(WIDE // 128):
                s0[q, b * block:(b + 1) * block, :] = piece[:, q * 128:(q + 1) * 128]
    else:
        for q in range(WIDE // 128):
            s0[q] = x_ref[:, q * 128:(q + 1) * 128].astype(jnp.float32)
    bufs = (s0, s1)
    for index, (kind, bits) in enumerate(levels):
        src = bufs[index % 2]
        dst = bufs[(index + 1) % 2]
        count = 4 if kind == "quad" else 2
        w_ref = w_refs[0] if kind == "quad" else w_refs[-1]
        children = [load_class(src, class_bits(bits, c)).astype(jnp.bfloat16) for c in range(count)]
        stacked = jnp.concatenate(children, 1)
        for t in range(count):
            fixed = class_bits(bits, t)
            y = lax.dot_general(
                stacked, w_ref[t], (((1,), (1,)), ((), ())), preferred_element_type=jnp.float32
            )
            lane = lax.broadcasted_iota(jnp.int32, y.shape, 1)
            swapped = jnp.where(lane < P_SIZE, pltpu.roll(y, WIDE - P_SIZE, 1), pltpu.roll(y, P_SIZE, 1))
            cs = load_class(cos_ref, fixed)
            sn = load_class(sin_ref, fixed)
            out = (y * cs + swapped * sn).astype(jnp.bfloat16).astype(jnp.float32)
            store_class(dst, fixed, out)
    last = bufs[len(levels) % 2]
    total = None
    pad = jnp.zeros((block, 4 * F - WIDE), jnp.float32)
    for b in range(4):
        piece = jnp.concatenate([last[q, b * block:(b + 1) * block, :] for q in range(WIDE // 128)], 1)
        piece = jnp.concatenate([piece, pad], 1)
        if b:
            piece = pltpu.roll(piece, b * F, 1)
        total = piece if total is None else total + piece
    o_ref[...] = total.astype(o_ref.dtype)


def run_levels(levels, packed_in, x, f_t, m_list):
    rows = 1024
    vmem = pl.BlockSpec(memory_space=pltpu.VMEM)
    w_scratch = [
        pltpu.VMEM((m.shape[0], WIDE, m.shape[1] * WIDE), jnp.bfloat16) for m in m_list
    ]
    m_list = [jnp.pad(m, [(0, 0)] * 4 + [(0, LANE - P_SIZE)]) for m in m_list]
    return pl.pallas_call(
        functools.partial(levels_kernel, levels, packed_in),
        out_shape=jax.ShapeDtypeStruct((rows // 4, 4 * F), jnp.bfloat16),
        in_specs=[vmem] * (2 + len(m_list)),
        out_specs=vmem,
        scratch_shapes=[pltpu.VMEM((WIDE // 128, rows, 128), jnp.float32)] * 4 + w_scratch,
        compiler_params=pltpu.CompilerParams(vmem_limit_bytes=60 * 1024 * 1024),
    )(x, f_t, *m_list)


def bits_of(value, count):
    return [(value >> k) & 1 for k in range(count)]


def factors(slope, a, b):
    center_x = (a.astype(jnp.float32) + 0.5) / 256.0 - 0.5
    center_y = (b.astype(jnp.float32) + 0.5) / 1024.0 - 0.5
    part_a = slope[0][None, :] * center_x[:, None]
    part_b = slope[1][None, :] * center_y[:, None]
    pad = [(0, 0), (0, WIDE - F)]

    def lanes(v):
        return jnp.pad(jnp.concatenate([v, v], 1), pad)

    return jnp.stack([lanes(jnp.cos(part_a)), lanes(jnp.sin(part_a)), lanes(jnp.cos(part_b)), lanes(jnp.sin(part_b))])


def build_tables(cos_ref, sin_ref, f_ref):
    groups = f_ref.shape[1]
    cb = f_ref[2]
    sb = f_ref[3]
    lane = lax.broadcasted_iota(jnp.int32, cb.shape, 1)
    for i in range(groups):
        ca = f_ref[0, i:i + 1, :]
        sa = f_ref[1, i:i + 1, :]
        cosine = ca * cb - sa * sb
        sine = sa * cb + ca * sb
        sine = jnp.where(lane < P_SIZE, -sine, sine)
        rows = pl.ds(i * groups, groups)
        for q in range(WIDE // 128):
            cos_ref[q, rows, :] = cosine[:, q * 128:(q + 1) * 128]
            sin_ref[q, rows, :] = sine[:, q * 128:(q + 1) * 128]


def exchange(z):
    shape = z.shape
    z = z.transpose(0, 1, 4, 2, 3, 5).reshape(shape[0] * shape[1], 2, -1)
    z = lax.all_to_all(z, ("gx", "gy"), 0, 0, tiled=True)
    z = z.reshape(shape[0], shape[1], 2, 2, 2, shape[5])
    return z.transpose(0, 1, 3, 4, 2, 5)


def exchange2(y):
    lanes = y.shape[1]
    cut = 512
    first = y[:, :cut].reshape(8, 32, cut)
    second = y[:, cut:].reshape(8, 32, lanes - cut)
    first = lax.all_to_all(first, "gx", 0, 0, tiled=True)
    second = lax.all_to_all(second, "gy", 1, 1, tiled=True)
    first = lax.all_to_all(first, "gy", 1, 1, tiled=True)
    second = lax.all_to_all(second, "gx", 0, 0, tiled=True)
    return jnp.concatenate([first.reshape(256, cut), second.reshape(256, lanes - cut)], 1)


def local(source, slope, quad, pair):
    place_x = lax.axis_index("gx")
    place_y = lax.axis_index("gy")
    wq = quad.reshape(4, 4, 2, P_SIZE, P_SIZE)
    wp = pair.reshape(2, 2, 2, P_SIZE, P_SIZE)
    group = jnp.arange(32, dtype=jnp.int32)

    f1 = factors(slope, place_x * 32 + group, place_y * 32 + group)
    x = source.reshape(F, 1024).T
    x = jnp.pad(x, [(0, 0), (0, WIDE - F)])
    levels1 = [("quad", (k + 5, k)) for k in range(5)]
    y1 = run_levels(levels1, False, x, f1, [wq])
    z = exchange2(y1)
    a2 = place_x + 8 * ((group >> 3) & 1) + 16 * ((group >> 4) & 1) + 32 * (group & 7)
    b2 = place_y + 32 * group
    f2 = factors(slope, a2, b2)
    levels2 = [("quad", (5, 0)), ("quad", (6, 1)), ("quad", (7, 2)), ("pair", (3,)), ("pair", (4,))]
    y2 = run_levels(levels2, True, z, f2, [wq, wp])
    w = exchange2(y2)
    w = w.reshape(256, 4, F).transpose(2, 1, 0)
    return w.reshape(F, 1, 1, 1024)


def solution(mesh):
    in_specs = (P(None, "gx", "gy", None), P(), P(), P())
    out_specs = P(None, "gx", "gy", None)
    return jax.shard_map(local, mesh=mesh, in_specs=in_specs, out_specs=out_specs, check_vma=False)
```

```python
import functools

import jax
import jax.numpy as jnp
from jax import lax
from jax.experimental import pallas as pl
from jax.experimental.pallas import tpu as pltpu
from jax.sharding import PartitionSpec as P

P_SIZE = 144
SIDE = 32
LANE = 256
WIDE = 384
F = 2 * P_SIZE


def padded(x):
    x = x.reshape(x.shape[:-2] + (F,))
    pad = [(0, 0)] * (x.ndim - 1) + [(0, WIDE - F)]
    return jnp.pad(x, pad)


def build_weights(wt_ref, m_ref):
    count = wt_ref.shape[0]
    zeros = jnp.zeros((P_SIZE, 128), jnp.float32)

    def ext(v):
        return jnp.concatenate([v, zeros], 1)

    for t in range(count):
        wt_ref[t, F:WIDE, :] = jnp.zeros((WIDE - F, wt_ref.shape[2]), wt_ref.dtype)
        for c in range(count):
            real = ext(m_ref[t, c, 0].astype(jnp.float32))
            imag = ext(m_ref[t, c, 1].astype(jnp.float32))
            top = real + pltpu.roll(-imag, P_SIZE, 1)
            bottom = imag + pltpu.roll(real, P_SIZE, 1)
            base = c * WIDE
            wt_ref[t, 0:P_SIZE, base:base + WIDE] = top.astype(wt_ref.dtype)
            wt_ref[t, P_SIZE:F, base:base + WIDE] = bottom.astype(wt_ref.dtype)


def class_pieces(fixed, rows):
    low = min(fixed)
    base = sum(v << p for p, v in fixed.items())
    free = [p for p in range(rows.bit_length() - 1) if p not in fixed]
    if (1 << low) >= 8:
        outer = [p for p in free if p > low]
        starts = []
        for k in range(1 << len(outer)):
            starts.append(base + sum(((k >> i) & 1) << p for i, p in enumerate(outer)))
        return [pl.ds(st, 1 << low) for st in starts]
    above = [p for p in fixed if p > low]
    top = min(above) if above else rows.bit_length() - 1
    inner = [p for p in free if low < p < top]
    outer = [p for p in free if p < low or p > top]
    slices = []
    for k in range(1 << len(outer)):
        st = base + sum(((k >> i) & 1) << p for i, p in enumerate(outer))
        slices.append(pl.ds(st, 1 << len(inner), stride=1 << (low + 1)))
    return slices


def load_class(ref, fixed):
    chunks, rows = ref.shape[:2]
    pieces = []
    for s in class_pieces(fixed, rows):
        parts = [ref[q, s, :] for q in range(chunks)]
        pieces.append(jnp.concatenate(parts, 1))
    return pieces[0] if len(pieces) == 1 else jnp.concatenate(pieces, 0)


def store_class(ref, fixed, value):
    chunks, rows = ref.shape[:2]
    at = 0
    for s in class_pieces(fixed, rows):
        size = s.size
        for q in range(chunks):
            ref[q, s, :] = value[at:at + size, q * 128:(q + 1) * 128]
        at += size


def class_bits(bits, c):
    if len(bits) == 2:
        return {bits[0]: c >> 1, bits[1]: c & 1}
    return {bits[0]: c}


def levels_kernel(levels, packed_in, x_ref, f_ref, *refs):
    count_w = (len(refs) - 5) // 2
    m_refs = refs[:count_w]
    o_ref, s0, s1, cos_ref, sin_ref = refs[count_w:count_w + 5]
    w_refs = refs[count_w + 5:]
    build_tables(cos_ref, sin_ref, f_ref)
    for w_ref, m_ref in zip(w_refs, m_refs):
        build_weights(w_ref, m_ref)
    rows = s0.shape[1]
    block = rows // 4
    if packed_in:
        lane = lax.broadcasted_iota(jnp.int32, (block, WIDE), 1)
        parts = []
        for r in range(2):
            v = x_ref[:, r, :].astype(jnp.float32)
            parts.append(jnp.concatenate([v, jnp.zeros((block, 640 - 4 * P_SIZE), jnp.float32)], 1))
        for b in range(4):
            re = pltpu.roll(parts[0], (640 - b * P_SIZE) % 640, 1)[:, :WIDE]
            im = pltpu.roll(parts[1], (640 + P_SIZE - b * P_SIZE) % 640, 1)[:, :WIDE]
            piece = jnp.where(lane < P_SIZE, re, jnp.where(lane < F, im, 0.0))
            for q in range(WIDE // 128):
                s0[q, b * block:(b + 1) * block, :] = piece[:, q * 128:(q + 1) * 128]
    else:
        for q in range(WIDE // 128):
            s0[q] = x_ref[:, q * 128:(q + 1) * 128].astype(jnp.float32)
    bufs = (s0, s1)
    for index, (kind, bits) in enumerate(levels):
        src = bufs[index % 2]
        dst = bufs[(index + 1) % 2]
        count = 4 if kind == "quad" else 2
        w_ref = w_refs[0] if kind == "quad" else w_refs[-1]
        children = [load_class(src, class_bits(bits, c)).astype(jnp.bfloat16) for c in range(count)]
        stacked = jnp.concatenate(children, 1)
        for t in range(count):
            fixed = class_bits(bits, t)
            y = lax.dot_general(
                stacked, w_ref[t], (((1,), (1,)), ((), ())), preferred_element_type=jnp.float32
            )
            lane = lax.broadcasted_iota(jnp.int32, y.shape, 1)
            swapped = jnp.where(lane < P_SIZE, pltpu.roll(y, WIDE - P_SIZE, 1), pltpu.roll(y, P_SIZE, 1))
            cs = load_class(cos_ref, fixed)
            sn = load_class(sin_ref, fixed)
            out = (y * cs + swapped * sn).astype(jnp.bfloat16).astype(jnp.float32)
            store_class(dst, fixed, out)
    last = bufs[len(levels) % 2]
    lane = lax.broadcasted_iota(jnp.int32, (block, 640), 1)
    pad = jnp.zeros((block, 640 - WIDE), jnp.float32)
    totals = [None, None]
    for b in range(4):
        piece = jnp.concatenate([last[q, b * block:(b + 1) * block, :] for q in range(WIDE // 128)], 1)
        piece = jnp.concatenate([piece, pad], 1)
        re = jnp.where(lane < P_SIZE, piece, 0.0)
        im = jnp.where((lane >= P_SIZE) & (lane < F), piece, 0.0)
        if b:
            re = pltpu.roll(re, b * P_SIZE, 1)
        im = pltpu.roll(im, (640 + b * P_SIZE - P_SIZE) % 640, 1)
        totals[0] = re if totals[0] is None else totals[0] + re
        totals[1] = im if totals[1] is None else totals[1] + im
    for r in range(2):
        o_ref[:, r, :] = totals[r][:, :4 * P_SIZE].astype(o_ref.dtype)


def run_levels(levels, packed_in, x, f_t, m_list):
    rows = 1024
    vmem = pl.BlockSpec(memory_space=pltpu.VMEM)
    w_scratch = [
        pltpu.VMEM((m.shape[0], WIDE, m.shape[1] * WIDE), jnp.bfloat16) for m in m_list
    ]
    m_list = [jnp.pad(m, [(0, 0)] * 4 + [(0, LANE - P_SIZE)]) for m in m_list]
    return pl.pallas_call(
        functools.partial(levels_kernel, levels, packed_in),
        out_shape=jax.ShapeDtypeStruct((rows // 4, 2, 4 * P_SIZE), jnp.bfloat16),
        in_specs=[vmem] * (2 + len(m_list)),
        out_specs=vmem,
        scratch_shapes=[pltpu.VMEM((WIDE // 128, rows, 128), jnp.float32)] * 4 + w_scratch,
        compiler_params=pltpu.CompilerParams(vmem_limit_bytes=60 * 1024 * 1024),
    )(x, f_t, *m_list)


def bits_of(value, count):
    return [(value >> k) & 1 for k in range(count)]


def factors(slope, a, b):
    center_x = (a.astype(jnp.float32) + 0.5) / 256.0 - 0.5
    center_y = (b.astype(jnp.float32) + 0.5) / 1024.0 - 0.5
    part_a = slope[0][None, :] * center_x[:, None]
    part_b = slope[1][None, :] * center_y[:, None]
    pad = [(0, 0), (0, WIDE - F)]

    def lanes(v):
        return jnp.pad(jnp.concatenate([v, v], 1), pad)

    return jnp.stack([lanes(jnp.cos(part_a)), lanes(jnp.sin(part_a)), lanes(jnp.cos(part_b)), lanes(jnp.sin(part_b))])


def build_tables(cos_ref, sin_ref, f_ref):
    groups = f_ref.shape[1]
    cb = f_ref[2]
    sb = f_ref[3]
    lane = lax.broadcasted_iota(jnp.int32, cb.shape, 1)
    for i in range(groups):
        ca = f_ref[0, i:i + 1, :]
        sa = f_ref[1, i:i + 1, :]
        cosine = ca * cb - sa * sb
        sine = sa * cb + ca * sb
        sine = jnp.where(lane < P_SIZE, -sine, sine)
        rows = pl.ds(i * groups, groups)
        for q in range(WIDE // 128):
            cos_ref[q, rows, :] = cosine[:, q * 128:(q + 1) * 128]
            sin_ref[q, rows, :] = sine[:, q * 128:(q + 1) * 128]


def exchange(z):
    shape = z.shape
    z = z.transpose(0, 1, 4, 2, 3, 5).reshape(shape[0] * shape[1], 2, -1)
    z = lax.all_to_all(z, ("gx", "gy"), 0, 0, tiled=True)
    z = z.reshape(shape[0], shape[1], 2, 2, 2, shape[5])
    return z.transpose(0, 1, 3, 4, 2, 5)


def local(source, slope, quad, pair):
    place_x = lax.axis_index("gx")
    place_y = lax.axis_index("gy")
    wq = quad.reshape(4, 4, 2, P_SIZE, P_SIZE)
    wp = pair.reshape(2, 2, 2, P_SIZE, P_SIZE)
    group = jnp.arange(32, dtype=jnp.int32)

    f1 = factors(slope, place_x * 32 + group, place_y * 32 + group)
    x = source.reshape(F, 1024).T
    x = jnp.pad(x, [(0, 0), (0, WIDE - F)])
    levels1 = [("quad", (k + 5, k)) for k in range(5)]
    y1 = run_levels(levels1, False, x, f1, [wq])
    z = lax.all_to_all(y1, ("gx", "gy"), 0, 0, tiled=True)
    a2 = place_x + 8 * ((group >> 3) & 1) + 16 * ((group >> 4) & 1) + 32 * (group & 7)
    b2 = place_y + 32 * group
    f2 = factors(slope, a2, b2)
    levels2 = [("quad", (5, 0)), ("quad", (6, 1)), ("quad", (7, 2)), ("pair", (3,)), ("pair", (4,))]
    y2 = run_levels(levels2, True, z, f2, [wq, wp])
    w = lax.all_to_all(y2, ("gx", "gy"), 0, 0, tiled=True)
    w = w.reshape(256, 2, 4, P_SIZE).transpose(1, 3, 2, 0)
    return w.reshape(F, 1, 1, 1024)


def solution(mesh):
    in_specs = (P(None, "gx", "gy", None), P(), P(), P())
    out_specs = P(None, "gx", "gy", None)
    return jax.shard_map(local, mesh=mesh, in_specs=in_specs, out_specs=out_specs, check_vma=False)
```

```python
import functools

import jax
import jax.numpy as jnp
from jax import lax
from jax.experimental import pallas as pl
from jax.experimental.pallas import tpu as pltpu
from jax.sharding import PartitionSpec as P

P_SIZE = 144
SIDE = 32
LANE = 256
WIDE = 384
F = 2 * P_SIZE


def padded(x):
    x = x.reshape(x.shape[:-2] + (F,))
    pad = [(0, 0)] * (x.ndim - 1) + [(0, WIDE - F)]
    return jnp.pad(x, pad)


def build_weights(wt_ref, m_ref):
    count = wt_ref.shape[0]
    zeros = jnp.zeros((P_SIZE, 128), jnp.float32)

    def ext(v):
        return jnp.concatenate([v, zeros], 1)

    for t in range(count):
        wt_ref[t, F:WIDE, :] = jnp.zeros((WIDE - F, wt_ref.shape[2]), wt_ref.dtype)
        for c in range(count):
            real = ext(m_ref[t, c, 0].astype(jnp.float32))
            imag = ext(m_ref[t, c, 1].astype(jnp.float32))
            top = real + pltpu.roll(-imag, P_SIZE, 1)
            bottom = imag + pltpu.roll(real, P_SIZE, 1)
            base = c * WIDE
            wt_ref[t, 0:P_SIZE, base:base + WIDE] = top.astype(wt_ref.dtype)
            wt_ref[t, P_SIZE:F, base:base + WIDE] = bottom.astype(wt_ref.dtype)


def class_pieces(fixed, rows):
    low = min(fixed)
    base = sum(v << p for p, v in fixed.items())
    free = [p for p in range(rows.bit_length() - 1) if p not in fixed]
    if (1 << low) >= 8 and len(fixed) > 1:
        outer = [p for p in free if p > low]
        starts = []
        for k in range(1 << len(outer)):
            starts.append(base + sum(((k >> i) & 1) << p for i, p in enumerate(outer)))
        return [pl.ds(st, 1 << low) for st in starts]
    above = [p for p in fixed if p > low]
    top = min(above) if above else rows.bit_length() - 1
    inner = [p for p in free if low < p < top]
    outer = [p for p in free if p < low or p > top]
    slices = []
    for k in range(1 << len(outer)):
        st = base + sum(((k >> i) & 1) << p for i, p in enumerate(outer))
        slices.append(pl.ds(st, 1 << len(inner), stride=1 << (low + 1)))
    return slices


def load_class(ref, fixed):
    chunks, rows = ref.shape[:2]
    pieces = []
    for s in class_pieces(fixed, rows):
        parts = [ref[q, s, :] for q in range(chunks)]
        pieces.append(jnp.concatenate(parts, 1))
    return pieces[0] if len(pieces) == 1 else jnp.concatenate(pieces, 0)


def store_class(ref, fixed, value):
    chunks, rows = ref.shape[:2]
    at = 0
    for s in class_pieces(fixed, rows):
        size = s.size
        for q in range(chunks):
            ref[q, s, :] = value[at:at + size, q * 128:(q + 1) * 128]
        at += size


def class_bits(bits, c):
    if len(bits) == 2:
        return {bits[0]: c >> 1, bits[1]: c & 1}
    return {bits[0]: c}


def levels_kernel(levels, packed_in, x_ref, f_ref, *refs):
    count_w = (len(refs) - 5) // 2
    m_refs = refs[:count_w]
    o_ref, s0, s1, cos_ref, sin_ref = refs[count_w:count_w + 5]
    w_refs = refs[count_w + 5:]
    build_tables(cos_ref, sin_ref, f_ref)
    for w_ref, m_ref in zip(w_refs, m_refs):
        build_weights(w_ref, m_ref)
    rows = s0.shape[1]
    block = rows // 4
    if packed_in:
        lane = lax.broadcasted_iota(jnp.int32, (block, WIDE), 1)
        parts = []
        for r in range(2):
            v = x_ref[:, r, :].astype(jnp.float32)
            parts.append(jnp.concatenate([v, jnp.zeros((block, 640 - 4 * P_SIZE), jnp.float32)], 1))
        for b in range(4):
            re = pltpu.roll(parts[0], (640 - b * P_SIZE) % 640, 1)[:, :WIDE]
            im = pltpu.roll(parts[1], (640 + P_SIZE - b * P_SIZE) % 640, 1)[:, :WIDE]
            piece = jnp.where(lane < P_SIZE, re, jnp.where(lane < F, im, 0.0))
            for q in range(WIDE // 128):
                s0[q, b * block:(b + 1) * block, :] = piece[:, q * 128:(q + 1) * 128]
    else:
        v = x_ref[...].astype(jnp.float32)
        v = jnp.concatenate([v, jnp.zeros((WIDE - F, rows), jnp.float32)], 0).T
        for q in range(WIDE // 128):
            s0[q] = v[:, q * 128:(q + 1) * 128]
    bufs = (s0, s1)
    for index, (kind, bits) in enumerate(levels):
        src = bufs[index % 2]
        dst = bufs[(index + 1) % 2]
        count = 4 if kind == "quad" else 2
        w_ref = w_refs[0] if kind == "quad" else w_refs[-1]
        children = [load_class(src, class_bits(bits, c)).astype(jnp.bfloat16) for c in range(count)]
        stacked = jnp.concatenate(children, 1)
        for t in range(count):
            fixed = class_bits(bits, t)
            y = lax.dot_general(
                stacked, w_ref[t], (((1,), (1,)), ((), ())), preferred_element_type=jnp.float32
            )
            lane = lax.broadcasted_iota(jnp.int32, y.shape, 1)
            swapped = jnp.where(lane < P_SIZE, pltpu.roll(y, WIDE - P_SIZE, 1), pltpu.roll(y, P_SIZE, 1))
            cs = load_class(cos_ref, fixed)
            sn = load_class(sin_ref, fixed)
            out = (y * cs + swapped * sn).astype(jnp.bfloat16).astype(jnp.float32)
            store_class(dst, fixed, out)
    last = bufs[len(levels) % 2]
    lane = lax.broadcasted_iota(jnp.int32, (block, 640), 1)
    pad = jnp.zeros((block, 640 - WIDE), jnp.float32)
    totals = [None, None]
    for b in range(4):
        piece = jnp.concatenate([last[q, b * block:(b + 1) * block, :] for q in range(WIDE // 128)], 1)
        piece = jnp.concatenate([piece, pad], 1)
        re = jnp.where(lane < P_SIZE, piece, 0.0)
        im = jnp.where((lane >= P_SIZE) & (lane < F), piece, 0.0)
        if b:
            re = pltpu.roll(re, b * P_SIZE, 1)
        im = pltpu.roll(im, (640 + b * P_SIZE - P_SIZE) % 640, 1)
        totals[0] = re if totals[0] is None else totals[0] + re
        totals[1] = im if totals[1] is None else totals[1] + im
    for r in range(2):
        o_ref[:, r, :] = totals[r][:, :4 * P_SIZE].astype(o_ref.dtype)


def run_levels(levels, packed_in, x, f_t, m_list):
    rows = 1024
    vmem = pl.BlockSpec(memory_space=pltpu.VMEM)
    w_scratch = [
        pltpu.VMEM((m.shape[0], WIDE, m.shape[1] * WIDE), jnp.bfloat16) for m in m_list
    ]
    m_list = [jnp.pad(m, [(0, 0)] * 4 + [(0, LANE - P_SIZE)]) for m in m_list]
    return pl.pallas_call(
        functools.partial(levels_kernel, levels, packed_in),
        out_shape=jax.ShapeDtypeStruct((rows // 4, 2, 4 * P_SIZE), jnp.bfloat16),
        in_specs=[vmem] * (2 + len(m_list)),
        out_specs=vmem,
        scratch_shapes=[pltpu.VMEM((WIDE // 128, rows, 128), jnp.float32)] * 4 + w_scratch,
        compiler_params=pltpu.CompilerParams(vmem_limit_bytes=60 * 1024 * 1024),
    )(x, f_t, *m_list)


def bits_of(value, count):
    return [(value >> k) & 1 for k in range(count)]


def factors(slope, a, b):
    center_x = (a.astype(jnp.float32) + 0.5) / 256.0 - 0.5
    center_y = (b.astype(jnp.float32) + 0.5) / 1024.0 - 0.5
    part_a = slope[0][None, :] * center_x[:, None]
    part_b = slope[1][None, :] * center_y[:, None]
    pad = [(0, 0), (0, WIDE - F)]

    def lanes(v):
        return jnp.pad(jnp.concatenate([v, v], 1), pad)

    return jnp.stack([lanes(jnp.cos(part_a)), lanes(jnp.sin(part_a)), lanes(jnp.cos(part_b)), lanes(jnp.sin(part_b))])


def build_tables(cos_ref, sin_ref, f_ref):
    groups = f_ref.shape[1]
    cb = f_ref[2]
    sb = f_ref[3]
    lane = lax.broadcasted_iota(jnp.int32, cb.shape, 1)
    for i in range(groups):
        ca = f_ref[0, i:i + 1, :]
        sa = f_ref[1, i:i + 1, :]
        cosine = ca * cb - sa * sb
        sine = sa * cb + ca * sb
        sine = jnp.where(lane < P_SIZE, -sine, sine)
        rows = pl.ds(i * groups, groups)
        for q in range(WIDE // 128):
            cos_ref[q, rows, :] = cosine[:, q * 128:(q + 1) * 128]
            sin_ref[q, rows, :] = sine[:, q * 128:(q + 1) * 128]


def exchange(z):
    shape = z.shape
    z = z.transpose(0, 1, 4, 2, 3, 5).reshape(shape[0] * shape[1], 2, -1)
    z = lax.all_to_all(z, ("gx", "gy"), 0, 0, tiled=True)
    z = z.reshape(shape[0], shape[1], 2, 2, 2, shape[5])
    return z.transpose(0, 1, 3, 4, 2, 5)


def local(source, slope, quad, pair):
    place_x = lax.axis_index("gx")
    place_y = lax.axis_index("gy")
    wq = quad.reshape(4, 4, 2, P_SIZE, P_SIZE)
    wp = pair.reshape(2, 2, 2, P_SIZE, P_SIZE)
    group = jnp.arange(32, dtype=jnp.int32)

    f1 = factors(slope, place_x * 32 + group, place_y * 32 + group)
    x = source.reshape(F, 1024)
    levels1 = [("quad", (k + 5, k)) for k in range(5)]
    y1 = run_levels(levels1, False, x, f1, [wq])
    z = lax.all_to_all(y1, ("gx", "gy"), 0, 0, tiled=True)
    a2 = place_x + 8 * ((group >> 3) & 1) + 16 * ((group >> 4) & 1) + 32 * (group & 7)
    b2 = place_y + 32 * group
    f2 = factors(slope, a2, b2)
    levels2 = [("quad", (5, 0)), ("quad", (6, 1)), ("quad", (7, 2)), ("pair", (3,)), ("pair", (4,))]
    y2 = run_levels(levels2, True, z, f2, [wq, wp])
    w = lax.all_to_all(y2, ("gx", "gy"), 0, 0, tiled=True)
    w = w.reshape(256, 2, 4, P_SIZE).transpose(1, 3, 2, 0)
    return w.reshape(F, 1, 1, 1024)


def solution(mesh):
    in_specs = (P(None, "gx", "gy", None), P(), P(), P())
    out_specs = P(None, "gx", "gy", None)
    return jax.shard_map(local, mesh=mesh, in_specs=in_specs, out_specs=out_specs, check_vma=False)
```

```python
import functools

import jax
import jax.numpy as jnp
from jax import lax
from jax.experimental import pallas as pl
from jax.experimental.pallas import tpu as pltpu
from jax.sharding import PartitionSpec as P

P_SIZE = 144
SIDE = 32
LANE = 256
WIDE = 384
F = 2 * P_SIZE


def padded(x):
    x = x.reshape(x.shape[:-2] + (F,))
    pad = [(0, 0)] * (x.ndim - 1) + [(0, WIDE - F)]
    return jnp.pad(x, pad)


def build_weights(wt_ref, m_ref):
    count = wt_ref.shape[0]
    zeros = jnp.zeros((P_SIZE, 128), jnp.float32)

    def ext(v):
        return jnp.concatenate([v, zeros], 1)

    for t in range(count):
        wt_ref[t, F:WIDE, :] = jnp.zeros((WIDE - F, wt_ref.shape[2]), wt_ref.dtype)
        for c in range(count):
            real = ext(m_ref[t, c, 0].astype(jnp.float32))
            imag = ext(m_ref[t, c, 1].astype(jnp.float32))
            top = real + pltpu.roll(-imag, P_SIZE, 1)
            bottom = imag + pltpu.roll(real, P_SIZE, 1)
            base = c * WIDE
            wt_ref[t, 0:P_SIZE, base:base + WIDE] = top.astype(wt_ref.dtype)
            wt_ref[t, P_SIZE:F, base:base + WIDE] = bottom.astype(wt_ref.dtype)


def class_pieces(fixed, rows):
    low = min(fixed)
    base = sum(v << p for p, v in fixed.items())
    free = [p for p in range(rows.bit_length() - 1) if p not in fixed]
    if (1 << low) >= 8:
        outer = [p for p in free if p > low]
        starts = []
        for k in range(1 << len(outer)):
            starts.append(base + sum(((k >> i) & 1) << p for i, p in enumerate(outer)))
        return [pl.ds(st, 1 << low) for st in starts]
    above = [p for p in fixed if p > low]
    top = min(above) if above else rows.bit_length() - 1
    inner = [p for p in free if low < p < top]
    outer = [p for p in free if p < low or p > top]
    slices = []
    for k in range(1 << len(outer)):
        st = base + sum(((k >> i) & 1) << p for i, p in enumerate(outer))
        slices.append(pl.ds(st, 1 << len(inner), stride=1 << (low + 1)))
    return slices


def load_class(ref, fixed):
    chunks, rows = ref.shape[:2]
    pieces = []
    for s in class_pieces(fixed, rows):
        parts = [ref[q, s, :] for q in range(chunks)]
        pieces.append(jnp.concatenate(parts, 1))
    return pieces[0] if len(pieces) == 1 else jnp.concatenate(pieces, 0)


def store_class(ref, fixed, value):
    chunks, rows = ref.shape[:2]
    at = 0
    for s in class_pieces(fixed, rows):
        size = s.size
        for q in range(chunks):
            ref[q, s, :] = value[at:at + size, q * 128:(q + 1) * 128]
        at += size


def class_bits(bits, c):
    if len(bits) == 2:
        return {bits[0]: c >> 1, bits[1]: c & 1}
    return {bits[0]: c}


def levels_kernel(levels, packed_in, x_ref, f_ref, *refs):
    count_w = (len(refs) - 5) // 2
    m_refs = refs[:count_w]
    o_ref, s0, s1, cos_ref, sin_ref = refs[count_w:count_w + 5]
    w_refs = refs[count_w + 5:]
    build_tables(cos_ref, sin_ref, f_ref)
    for w_ref, m_ref in zip(w_refs, m_refs):
        build_weights(w_ref, m_ref)
    rows = s0.shape[1]
    block = rows // 4
    if packed_in:
        lane = lax.broadcasted_iota(jnp.int32, (block, WIDE), 1)
        parts = []
        for r in range(2):
            v = x_ref[:, r, :].astype(jnp.float32)
            parts.append(jnp.concatenate([v, jnp.zeros((block, 640 - 4 * P_SIZE), jnp.float32)], 1))
        for b in range(4):
            re = pltpu.roll(parts[0], (640 - b * P_SIZE) % 640, 1)[:, :WIDE]
            im = pltpu.roll(parts[1], (640 + P_SIZE - b * P_SIZE) % 640, 1)[:, :WIDE]
            piece = jnp.where(lane < P_SIZE, re, jnp.where(lane < F, im, 0.0))
            for q in range(WIDE // 128):
                s0[q, b * block:(b + 1) * block, :] = piece[:, q * 128:(q + 1) * 128]
    else:
        v = x_ref[...].astype(jnp.float32)
        v = jnp.concatenate([v, jnp.zeros((WIDE - F, rows), jnp.float32)], 0).T
        for q in range(WIDE // 128):
            s0[q] = v[:, q * 128:(q + 1) * 128]
    bufs = (s0, s1)
    for index, (kind, bits) in enumerate(levels):
        src = bufs[index % 2]
        dst = bufs[(index + 1) % 2]
        count = 4 if kind == "quad" else 2
        w_ref = w_refs[0] if kind == "quad" else w_refs[-1]
        children = [load_class(src, class_bits(bits, c)).astype(jnp.bfloat16) for c in range(count)]
        stacked = jnp.concatenate(children, 1)
        for t in range(count):
            fixed = class_bits(bits, t)
            y = lax.dot_general(
                stacked, w_ref[t], (((1,), (1,)), ((), ())), preferred_element_type=jnp.float32
            )
            lane = lax.broadcasted_iota(jnp.int32, y.shape, 1)
            swapped = jnp.where(lane < P_SIZE, pltpu.roll(y, WIDE - P_SIZE, 1), pltpu.roll(y, P_SIZE, 1))
            cs = load_class(cos_ref, fixed)
            sn = load_class(sin_ref, fixed)
            out = (y * cs + swapped * sn).astype(jnp.bfloat16).astype(jnp.float32)
            store_class(dst, fixed, out)
    last = bufs[len(levels) % 2]
    lane = lax.broadcasted_iota(jnp.int32, (block, 640), 1)
    pad = jnp.zeros((block, 640 - WIDE), jnp.float32)
    totals = [None, None]
    for b in range(4):
        piece = jnp.concatenate([last[q, b * block:(b + 1) * block, :] for q in range(WIDE // 128)], 1)
        piece = jnp.concatenate([piece, pad], 1)
        re = jnp.where(lane < P_SIZE, piece, 0.0)
        im = jnp.where((lane >= P_SIZE) & (lane < F), piece, 0.0)
        if b:
            re = pltpu.roll(re, b * P_SIZE, 1)
        im = pltpu.roll(im, (640 + b * P_SIZE - P_SIZE) % 640, 1)
        totals[0] = re if totals[0] is None else totals[0] + re
        totals[1] = im if totals[1] is None else totals[1] + im
    for r in range(2):
        o_ref[:, r, :] = totals[r][:, :4 * P_SIZE].astype(o_ref.dtype)


def run_levels(levels, packed_in, x, f_t, m_list):
    rows = 1024
    vmem = pl.BlockSpec(memory_space=pltpu.VMEM)
    w_scratch = [
        pltpu.VMEM((m.shape[0], WIDE, m.shape[1] * WIDE), jnp.bfloat16) for m in m_list
    ]
    m_list = [jnp.pad(m, [(0, 0)] * 4 + [(0, LANE - P_SIZE)]) for m in m_list]
    return pl.pallas_call(
        functools.partial(levels_kernel, levels, packed_in),
        out_shape=jax.ShapeDtypeStruct((rows // 4, 2, 4 * P_SIZE), jnp.bfloat16),
        in_specs=[vmem] * (2 + len(m_list)),
        out_specs=vmem,
        scratch_shapes=[pltpu.VMEM((WIDE // 128, rows, 128), jnp.float32)] * 4 + w_scratch,
        compiler_params=pltpu.CompilerParams(vmem_limit_bytes=60 * 1024 * 1024),
    )(x, f_t, *m_list)


def bits_of(value, count):
    return [(value >> k) & 1 for k in range(count)]


def factors(slope, a, b):
    center_x = (a.astype(jnp.float32) + 0.5) / 256.0 - 0.5
    center_y = (b.astype(jnp.float32) + 0.5) / 1024.0 - 0.5
    part_a = slope[0][None, :] * center_x[:, None]
    part_b = slope[1][None, :] * center_y[:, None]
    pad = [(0, 0), (0, WIDE - F)]

    def lanes(v):
        return jnp.pad(jnp.concatenate([v, v], 1), pad)

    return jnp.stack([lanes(jnp.cos(part_a)), lanes(jnp.sin(part_a)), lanes(jnp.cos(part_b)), lanes(jnp.sin(part_b))])


def build_tables(cos_ref, sin_ref, f_ref):
    groups = f_ref.shape[1]
    cb = f_ref[2]
    sb = f_ref[3]
    lane = lax.broadcasted_iota(jnp.int32, cb.shape, 1)
    for i in range(groups):
        ca = f_ref[0, i:i + 1, :]
        sa = f_ref[1, i:i + 1, :]
        cosine = ca * cb - sa * sb
        sine = sa * cb + ca * sb
        sine = jnp.where(lane < P_SIZE, -sine, sine)
        rows = pl.ds(i * groups, groups)
        for q in range(WIDE // 128):
            cos_ref[q, rows, :] = cosine[:, q * 128:(q + 1) * 128]
            sin_ref[q, rows, :] = sine[:, q * 128:(q + 1) * 128]


def exchange(z):
    shape = z.shape
    z = z.transpose(0, 1, 4, 2, 3, 5).reshape(shape[0] * shape[1], 2, -1)
    z = lax.all_to_all(z, ("gx", "gy"), 0, 0, tiled=True)
    z = z.reshape(shape[0], shape[1], 2, 2, 2, shape[5])
    return z.transpose(0, 1, 3, 4, 2, 5)


def local(source, slope, quad, pair):
    place_x = lax.axis_index("gx")
    place_y = lax.axis_index("gy")
    wq = quad.reshape(4, 4, 2, P_SIZE, P_SIZE)
    wp = pair.reshape(2, 2, 2, P_SIZE, P_SIZE)
    group = jnp.arange(32, dtype=jnp.int32)

    f1 = factors(slope, place_x * 32 + group, place_y * 32 + group)
    x = source.reshape(F, 1024)
    levels1 = [("quad", (k + 5, k)) for k in range(5)]
    y1 = run_levels(levels1, False, x, f1, [wq])
    z = lax.all_to_all(y1, ("gx", "gy"), 0, 0, tiled=True)
    a2 = place_x + 8 * ((group >> 3) & 1) + 16 * ((group >> 4) & 1) + 32 * (group & 7)
    b2 = place_y + 32 * group
    f2 = factors(slope, a2, b2)
    levels2 = [("quad", (5, 0)), ("quad", (6, 1)), ("quad", (7, 2)), ("pair", (3,)), ("pair", (4,))]
    y2 = run_levels(levels2, True, z, f2, [wq, wp])
    w = lax.all_to_all(y2, ("gx", "gy"), 0, 0, tiled=True)
    w = w.reshape(256, 2, 4, P_SIZE).transpose(1, 3, 2, 0)
    return w.reshape(F, 1, 1, 1024)


def solution(mesh):
    in_specs = (P(None, "gx", "gy", None), P(), P(), P())
    out_specs = P(None, "gx", "gy", None)
    return jax.shard_map(local, mesh=mesh, in_specs=in_specs, out_specs=out_specs, check_vma=False)
```

```python
import functools

import jax
import jax.numpy as jnp
from jax import lax
from jax.experimental import pallas as pl
from jax.experimental.pallas import tpu as pltpu
from jax.sharding import PartitionSpec as P

P_SIZE = 144
SIDE = 32
LANE = 256
WIDE = 384
F = 2 * P_SIZE


def padded(x):
    x = x.reshape(x.shape[:-2] + (F,))
    pad = [(0, 0)] * (x.ndim - 1) + [(0, WIDE - F)]
    return jnp.pad(x, pad)


def build_weights(wt_ref, m_ref):
    count = wt_ref.shape[0]
    zeros = jnp.zeros((P_SIZE, 128), jnp.float32)

    def ext(v):
        return jnp.concatenate([v, zeros], 1)

    for t in range(count):
        wt_ref[t, F:WIDE, :] = jnp.zeros((WIDE - F, wt_ref.shape[2]), wt_ref.dtype)
        for c in range(count):
            real = ext(m_ref[t, c, 0].astype(jnp.float32))
            imag = ext(m_ref[t, c, 1].astype(jnp.float32))
            top = real + pltpu.roll(-imag, P_SIZE, 1)
            bottom = imag + pltpu.roll(real, P_SIZE, 1)
            base = c * WIDE
            wt_ref[t, 0:P_SIZE, base:base + WIDE] = top.astype(wt_ref.dtype)
            wt_ref[t, P_SIZE:F, base:base + WIDE] = bottom.astype(wt_ref.dtype)


def class_pieces(fixed, rows):
    low = min(fixed)
    base = sum(v << p for p, v in fixed.items())
    free = [p for p in range(rows.bit_length() - 1) if p not in fixed]
    if (1 << low) >= 8:
        outer = [p for p in free if p > low]
        starts = []
        for k in range(1 << len(outer)):
            starts.append(base + sum(((k >> i) & 1) << p for i, p in enumerate(outer)))
        return [pl.ds(st, 1 << low) for st in starts]
    above = [p for p in fixed if p > low]
    top = min(above) if above else rows.bit_length() - 1
    inner = [p for p in free if low < p < top]
    outer = [p for p in free if p < low or p > top]
    slices = []
    for k in range(1 << len(outer)):
        st = base + sum(((k >> i) & 1) << p for i, p in enumerate(outer))
        slices.append(pl.ds(st, 1 << len(inner), stride=1 << (low + 1)))
    return slices


def load_class(ref, fixed):
    chunks, rows = ref.shape[:2]
    pieces = []
    for s in class_pieces(fixed, rows):
        parts = [ref[q, s, :] for q in range(chunks)]
        pieces.append(jnp.concatenate(parts, 1))
    return pieces[0] if len(pieces) == 1 else jnp.concatenate(pieces, 0)


def store_class(ref, fixed, value):
    chunks, rows = ref.shape[:2]
    at = 0
    for s in class_pieces(fixed, rows):
        size = s.size
        for q in range(chunks):
            ref[q, s, :] = value[at:at + size, q * 128:(q + 1) * 128]
        at += size


def class_bits(bits, c):
    if len(bits) == 2:
        return {bits[0]: c >> 1, bits[1]: c & 1}
    return {bits[0]: c}


def levels_kernel(levels, packed_in, x_ref, f_ref, *refs):
    count_w = (len(refs) - 5) // 2
    m_refs = refs[:count_w]
    o_ref, s0, s1, cos_ref, sin_ref = refs[count_w:count_w + 5]
    w_refs = refs[count_w + 5:]
    build_tables(cos_ref, sin_ref, f_ref)
    for w_ref, m_ref in zip(w_refs, m_refs):
        build_weights(w_ref, m_ref)
    rows = s0.shape[1]
    block = rows // 4
    if packed_in:
        lane = lax.broadcasted_iota(jnp.int32, (block, WIDE), 1)
        parts = []
        for r in range(2):
            v = x_ref[:, r, :].astype(jnp.float32)
            parts.append(jnp.concatenate([v, jnp.zeros((block, 640 - 4 * P_SIZE), jnp.float32)], 1))
        for b in range(4):
            re = pltpu.roll(parts[0], (640 - b * P_SIZE) % 640, 1)[:, :WIDE]
            im = pltpu.roll(parts[1], (640 + P_SIZE - b * P_SIZE) % 640, 1)[:, :WIDE]
            piece = jnp.where(lane < P_SIZE, re, jnp.where(lane < F, im, 0.0))
            for q in range(WIDE // 128):
                s0[q, b * block:(b + 1) * block, :] = piece[:, q * 128:(q + 1) * 128]
    else:
        v = x_ref[...].astype(jnp.float32)
        v = jnp.concatenate([v, jnp.zeros((WIDE - F, rows), jnp.float32)], 0).T
        for q in range(WIDE // 128):
            s0[q] = v[:, q * 128:(q + 1) * 128]
    bufs = (s0, s1)
    for index, (kind, bits) in enumerate(levels):
        src = bufs[index % 2]
        dst = bufs[(index + 1) % 2]
        count = 4 if kind == "quad" else 2
        w_ref = w_refs[0] if kind == "quad" else w_refs[-1]
        children = [load_class(src, class_bits(bits, c)).astype(jnp.bfloat16) for c in range(count)]
        stacked = jnp.concatenate(children, 1)
        for t in range(count):
            fixed = class_bits(bits, t)
            y = lax.dot_general(
                stacked, w_ref[t], (((1,), (1,)), ((), ())), preferred_element_type=jnp.float32
            )
            lane = lax.broadcasted_iota(jnp.int32, y.shape, 1)
            swapped = jnp.where(lane < P_SIZE, pltpu.roll(y, WIDE - P_SIZE, 1), pltpu.roll(y, P_SIZE, 1))
            cs = load_class(cos_ref, fixed)
            sn = load_class(sin_ref, fixed)
            out = (y * cs + swapped * sn).astype(jnp.bfloat16).astype(jnp.float32)
            store_class(dst, fixed, out)
    last = bufs[len(levels) % 2]
    lane = lax.broadcasted_iota(jnp.int32, (block, 640), 1)
    pad = jnp.zeros((block, 640 - WIDE), jnp.float32)
    totals = [None, None]
    for b in range(4):
        piece = jnp.concatenate([last[q, b * block:(b + 1) * block, :] for q in range(WIDE // 128)], 1)
        piece = jnp.concatenate([piece, pad], 1)
        re = jnp.where(lane < P_SIZE, piece, 0.0)
        im = jnp.where((lane >= P_SIZE) & (lane < F), piece, 0.0)
        if b:
            re = pltpu.roll(re, b * P_SIZE, 1)
        im = pltpu.roll(im, (640 + b * P_SIZE - P_SIZE) % 640, 1)
        totals[0] = re if totals[0] is None else totals[0] + re
        totals[1] = im if totals[1] is None else totals[1] + im
    for r in range(2):
        o_ref[:, r, :] = totals[r][:, :4 * P_SIZE].astype(o_ref.dtype)


def run_levels(levels, packed_in, x, f_t, m_list):
    rows = 1024
    vmem = pl.BlockSpec(memory_space=pltpu.VMEM)
    w_scratch = [
        pltpu.VMEM((m.shape[0], WIDE, m.shape[1] * WIDE), jnp.bfloat16) for m in m_list
    ]
    m_list = [jnp.pad(m, [(0, 0)] * 4 + [(0, LANE - P_SIZE)]) for m in m_list]
    return pl.pallas_call(
        functools.partial(levels_kernel, levels, packed_in),
        out_shape=jax.ShapeDtypeStruct((rows // 4, 2, 4 * P_SIZE), jnp.bfloat16),
        in_specs=[vmem] * (2 + len(m_list)),
        out_specs=vmem,
        scratch_shapes=[pltpu.VMEM((WIDE // 128, rows, 128), jnp.float32)] * 4 + w_scratch,
        compiler_params=pltpu.CompilerParams(vmem_limit_bytes=60 * 1024 * 1024),
    )(x, f_t, *m_list)


def bits_of(value, count):
    return [(value >> k) & 1 for k in range(count)]


def factors(slope, a, b):
    center_x = (a.astype(jnp.float32) + 0.5) / 256.0 - 0.5
    center_y = (b.astype(jnp.float32) + 0.5) / 1024.0 - 0.5
    part_a = slope[0][None, :] * center_x[:, None]
    part_b = slope[1][None, :] * center_y[:, None]
    pad = [(0, 0), (0, WIDE - F)]

    def lanes(v):
        return jnp.pad(jnp.concatenate([v, v], 1), pad)

    return jnp.stack([lanes(jnp.cos(part_a)), lanes(jnp.sin(part_a)), lanes(jnp.cos(part_b)), lanes(jnp.sin(part_b))])


def build_tables(cos_ref, sin_ref, f_ref):
    groups = f_ref.shape[1]
    cb = f_ref[2]
    sb = f_ref[3]
    lane = lax.broadcasted_iota(jnp.int32, cb.shape, 1)
    for i in range(groups):
        ca = f_ref[0, i:i + 1, :]
        sa = f_ref[1, i:i + 1, :]
        cosine = ca * cb - sa * sb
        sine = sa * cb + ca * sb
        sine = jnp.where(lane < P_SIZE, -sine, sine)
        rows = pl.ds(i * groups, groups)
        for q in range(WIDE // 128):
            cos_ref[q, rows, :] = cosine[:, q * 128:(q + 1) * 128]
            sin_ref[q, rows, :] = sine[:, q * 128:(q + 1) * 128]


def exchange(z):
    shape = z.shape
    z = z.transpose(0, 1, 4, 2, 3, 5).reshape(shape[0] * shape[1], 2, -1)
    z = lax.all_to_all(z, ("gx", "gy"), 0, 0, tiled=True)
    z = z.reshape(shape[0], shape[1], 2, 2, 2, shape[5])
    return z.transpose(0, 1, 3, 4, 2, 5)


def local(source, slope, quad, pair):
    place_x = lax.axis_index("gx")
    place_y = lax.axis_index("gy")
    wq = lax.optimization_barrier(quad.astype(jnp.float32)).reshape(4, 4, 2, P_SIZE, P_SIZE)
    wp = pair.reshape(2, 2, 2, P_SIZE, P_SIZE)
    group = jnp.arange(32, dtype=jnp.int32)

    f1 = factors(slope, place_x * 32 + group, place_y * 32 + group)
    x = source.reshape(F, 1024)
    levels1 = [("quad", (k + 5, k)) for k in range(5)]
    y1 = run_levels(levels1, False, x, f1, [wq])
    z = lax.all_to_all(y1, ("gx", "gy"), 0, 0, tiled=True)
    a2 = place_x + 8 * ((group >> 3) & 1) + 16 * ((group >> 4) & 1) + 32 * (group & 7)
    b2 = place_y + 32 * group
    f2 = factors(slope, a2, b2)
    levels2 = [("quad", (5, 0)), ("quad", (6, 1)), ("quad", (7, 2)), ("pair", (3,)), ("pair", (4,))]
    y2 = run_levels(levels2, True, z, f2, [wq, wp])
    w = lax.all_to_all(y2, ("gx", "gy"), 0, 0, tiled=True)
    w = w.reshape(256, 2, 4, P_SIZE).transpose(1, 3, 2, 0)
    return w.reshape(F, 1, 1, 1024)


def solution(mesh):
    in_specs = (P(None, "gx", "gy", None), P(), P(), P())
    out_specs = P(None, "gx", "gy", None)
    return jax.shard_map(local, mesh=mesh, in_specs=in_specs, out_specs=out_specs, check_vma=False)
```

```python
import functools

import jax
import jax.numpy as jnp
from jax import lax
from jax.experimental import pallas as pl
from jax.experimental.pallas import tpu as pltpu
from jax.sharding import PartitionSpec as P

P_SIZE = 144
SIDE = 32
LANE = 256
WIDE = 384
F = 2 * P_SIZE


def padded(x):
    x = x.reshape(x.shape[:-2] + (F,))
    pad = [(0, 0)] * (x.ndim - 1) + [(0, WIDE - F)]
    return jnp.pad(x, pad)


def build_weights(wt_ref, m_ref):
    count = wt_ref.shape[0]
    row = lax.broadcasted_iota(jnp.int32, (P_SIZE, WIDE), 0)
    col = lax.broadcasted_iota(jnp.int32, (P_SIZE, WIDE), 1)
    first = (col == row).astype(jnp.bfloat16)
    second = (col == row + P_SIZE).astype(jnp.bfloat16)

    def place(v, sel):
        return jnp.dot(v, sel, preferred_element_type=jnp.float32)

    for t in range(count):
        wt_ref[t, F:WIDE, :] = jnp.zeros((WIDE - F, wt_ref.shape[2]), wt_ref.dtype)
        for c in range(count):
            real = m_ref[t, c, 0]
            imag = m_ref[t, c, 1]
            top = place(real, first) - place(imag, second)
            bottom = place(imag, first) + place(real, second)
            base = c * WIDE
            wt_ref[t, 0:P_SIZE, base:base + WIDE] = top.astype(wt_ref.dtype)
            wt_ref[t, P_SIZE:F, base:base + WIDE] = bottom.astype(wt_ref.dtype)


def class_pieces(fixed, rows):
    low = min(fixed)
    base = sum(v << p for p, v in fixed.items())
    free = [p for p in range(rows.bit_length() - 1) if p not in fixed]
    if (1 << low) >= 8:
        outer = [p for p in free if p > low]
        starts = []
        for k in range(1 << len(outer)):
            starts.append(base + sum(((k >> i) & 1) << p for i, p in enumerate(outer)))
        return [pl.ds(st, 1 << low) for st in starts]
    above = [p for p in fixed if p > low]
    top = min(above) if above else rows.bit_length() - 1
    inner = [p for p in free if low < p < top]
    outer = [p for p in free if p < low or p > top]
    slices = []
    for k in range(1 << len(outer)):
        st = base + sum(((k >> i) & 1) << p for i, p in enumerate(outer))
        slices.append(pl.ds(st, 1 << len(inner), stride=1 << (low + 1)))
    return slices


def load_class(ref, fixed):
    chunks, rows = ref.shape[:2]
    pieces = []
    for s in class_pieces(fixed, rows):
        parts = [ref[q, s, :] for q in range(chunks)]
        pieces.append(jnp.concatenate(parts, 1))
    return pieces[0] if len(pieces) == 1 else jnp.concatenate(pieces, 0)


def store_class(ref, fixed, value):
    chunks, rows = ref.shape[:2]
    at = 0
    for s in class_pieces(fixed, rows):
        size = s.size
        for q in range(chunks):
            ref[q, s, :] = value[at:at + size, q * 128:(q + 1) * 128]
        at += size


def class_bits(bits, c):
    if len(bits) == 2:
        return {bits[0]: c >> 1, bits[1]: c & 1}
    return {bits[0]: c}


def levels_kernel(levels, packed_in, x_ref, f_ref, *refs):
    count_w = (len(refs) - 5) // 2
    m_refs = refs[:count_w]
    o_ref, s0, s1, cos_ref, sin_ref = refs[count_w:count_w + 5]
    w_refs = refs[count_w + 5:]
    build_tables(cos_ref, sin_ref, f_ref)
    for w_ref, m_ref in zip(w_refs, m_refs):
        build_weights(w_ref, m_ref)
    rows = s0.shape[1]
    block = rows // 4
    if packed_in:
        lane = lax.broadcasted_iota(jnp.int32, (block, WIDE), 1)
        parts = []
        for r in range(2):
            v = x_ref[:, r, :].astype(jnp.float32)
            parts.append(jnp.concatenate([v, jnp.zeros((block, 640 - 4 * P_SIZE), jnp.float32)], 1))
        for b in range(4):
            re = pltpu.roll(parts[0], (640 - b * P_SIZE) % 640, 1)[:, :WIDE]
            im = pltpu.roll(parts[1], (640 + P_SIZE - b * P_SIZE) % 640, 1)[:, :WIDE]
            piece = jnp.where(lane < P_SIZE, re, jnp.where(lane < F, im, 0.0))
            for q in range(WIDE // 128):
                s0[q, b * block:(b + 1) * block, :] = piece[:, q * 128:(q + 1) * 128]
    else:
        v = x_ref[...].astype(jnp.float32)
        v = jnp.concatenate([v, jnp.zeros((WIDE - F, rows), jnp.float32)], 0).T
        for q in range(WIDE // 128):
            s0[q] = v[:, q * 128:(q + 1) * 128]
    bufs = (s0, s1)
    for index, (kind, bits) in enumerate(levels):
        src = bufs[index % 2]
        dst = bufs[(index + 1) % 2]
        count = 4 if kind == "quad" else 2
        w_ref = w_refs[0] if kind == "quad" else w_refs[-1]
        children = [load_class(src, class_bits(bits, c)).astype(jnp.bfloat16) for c in range(count)]
        stacked = jnp.concatenate(children, 1)
        for t in range(count):
            fixed = class_bits(bits, t)
            y = lax.dot_general(
                stacked, w_ref[t], (((1,), (1,)), ((), ())), preferred_element_type=jnp.float32
            )
            lane = lax.broadcasted_iota(jnp.int32, y.shape, 1)
            swapped = jnp.where(lane < P_SIZE, pltpu.roll(y, WIDE - P_SIZE, 1), pltpu.roll(y, P_SIZE, 1))
            cs = load_class(cos_ref, fixed)
            sn = load_class(sin_ref, fixed)
            out = (y * cs + swapped * sn).astype(jnp.bfloat16).astype(jnp.float32)
            store_class(dst, fixed, out)
    last = bufs[len(levels) % 2]
    lane = lax.broadcasted_iota(jnp.int32, (block, 640), 1)
    pad = jnp.zeros((block, 640 - WIDE), jnp.float32)
    totals = [None, None]
    for b in range(4):
        piece = jnp.concatenate([last[q, b * block:(b + 1) * block, :] for q in range(WIDE // 128)], 1)
        piece = jnp.concatenate([piece, pad], 1)
        re = jnp.where(lane < P_SIZE, piece, 0.0)
        im = jnp.where((lane >= P_SIZE) & (lane < F), piece, 0.0)
        if b:
            re = pltpu.roll(re, b * P_SIZE, 1)
        im = pltpu.roll(im, (640 + b * P_SIZE - P_SIZE) % 640, 1)
        totals[0] = re if totals[0] is None else totals[0] + re
        totals[1] = im if totals[1] is None else totals[1] + im
    for r in range(2):
        o_ref[:, r, :] = totals[r][:, :4 * P_SIZE].astype(o_ref.dtype)


def run_levels(levels, packed_in, x, f_t, m_list):
    rows = 1024
    vmem = pl.BlockSpec(memory_space=pltpu.VMEM)
    w_scratch = [
        pltpu.VMEM((m.shape[0], WIDE, m.shape[1] * WIDE), jnp.bfloat16) for m in m_list
    ]
    return pl.pallas_call(
        functools.partial(levels_kernel, levels, packed_in),
        out_shape=jax.ShapeDtypeStruct((rows // 4, 2, 4 * P_SIZE), jnp.bfloat16),
        in_specs=[vmem] * (2 + len(m_list)),
        out_specs=vmem,
        scratch_shapes=[pltpu.VMEM((WIDE // 128, rows, 128), jnp.float32)] * 4 + w_scratch,
        compiler_params=pltpu.CompilerParams(vmem_limit_bytes=60 * 1024 * 1024),
    )(x, f_t, *m_list)


def bits_of(value, count):
    return [(value >> k) & 1 for k in range(count)]


def factors(slope, a, b):
    center_x = (a.astype(jnp.float32) + 0.5) / 256.0 - 0.5
    center_y = (b.astype(jnp.float32) + 0.5) / 1024.0 - 0.5
    part_a = slope[0][None, :] * center_x[:, None]
    part_b = slope[1][None, :] * center_y[:, None]
    pad = [(0, 0), (0, WIDE - F)]

    def lanes(v):
        return jnp.pad(jnp.concatenate([v, v], 1), pad)

    return jnp.stack([lanes(jnp.cos(part_a)), lanes(jnp.sin(part_a)), lanes(jnp.cos(part_b)), lanes(jnp.sin(part_b))])


def build_tables(cos_ref, sin_ref, f_ref):
    groups = f_ref.shape[1]
    cb = f_ref[2]
    sb = f_ref[3]
    lane = lax.broadcasted_iota(jnp.int32, cb.shape, 1)
    for i in range(groups):
        ca = f_ref[0, i:i + 1, :]
        sa = f_ref[1, i:i + 1, :]
        cosine = ca * cb - sa * sb
        sine = sa * cb + ca * sb
        sine = jnp.where(lane < P_SIZE, -sine, sine)
        rows = pl.ds(i * groups, groups)
        for q in range(WIDE // 128):
            cos_ref[q, rows, :] = cosine[:, q * 128:(q + 1) * 128]
            sin_ref[q, rows, :] = sine[:, q * 128:(q + 1) * 128]


def exchange(z):
    shape = z.shape
    z = z.transpose(0, 1, 4, 2, 3, 5).reshape(shape[0] * shape[1], 2, -1)
    z = lax.all_to_all(z, ("gx", "gy"), 0, 0, tiled=True)
    z = z.reshape(shape[0], shape[1], 2, 2, 2, shape[5])
    return z.transpose(0, 1, 3, 4, 2, 5)


def local(source, slope, quad, pair):
    place_x = lax.axis_index("gx")
    place_y = lax.axis_index("gy")
    wq = quad.reshape(4, 4, 2, P_SIZE, P_SIZE)
    wp = pair.reshape(2, 2, 2, P_SIZE, P_SIZE)
    group = jnp.arange(32, dtype=jnp.int32)

    f1 = factors(slope, place_x * 32 + group, place_y * 32 + group)
    x = source.reshape(F, 1024)
    levels1 = [("quad", (k + 5, k)) for k in range(5)]
    y1 = run_levels(levels1, False, x, f1, [wq])
    z = lax.all_to_all(y1, ("gx", "gy"), 0, 0, tiled=True)
    a2 = place_x + 8 * ((group >> 3) & 1) + 16 * ((group >> 4) & 1) + 32 * (group & 7)
    b2 = place_y + 32 * group
    f2 = factors(slope, a2, b2)
    levels2 = [("quad", (5, 0)), ("quad", (6, 1)), ("quad", (7, 2)), ("pair", (3,)), ("pair", (4,))]
    y2 = run_levels(levels2, True, z, f2, [wq, wp])
    w = lax.all_to_all(y2, ("gx", "gy"), 0, 0, tiled=True)
    w = w.reshape(256, 2, 4, P_SIZE).transpose(1, 3, 2, 0)
    return w.reshape(F, 1, 1, 1024)


def solution(mesh):
    in_specs = (P(None, "gx", "gy", None), P(), P(), P())
    out_specs = P(None, "gx", "gy", None)
    return jax.shard_map(local, mesh=mesh, in_specs=in_specs, out_specs=out_specs, check_vma=False)
```

```python
import functools

import jax
import jax.numpy as jnp
from jax import lax
from jax.experimental import pallas as pl
from jax.experimental.pallas import tpu as pltpu
from jax.sharding import PartitionSpec as P

P_SIZE = 144
SIDE = 32
LANE = 256
WIDE = 384
F = 2 * P_SIZE


def padded(x):
    x = x.reshape(x.shape[:-2] + (F,))
    pad = [(0, 0)] * (x.ndim - 1) + [(0, WIDE - F)]
    return jnp.pad(x, pad)


def build_weights(wt_ref, m_ref):
    count = wt_ref.shape[0]
    zeros = jnp.zeros((P_SIZE, 128), jnp.float32)

    def ext(v):
        return jnp.concatenate([v, zeros], 1)

    for t in range(count):
        wt_ref[t, F:WIDE, :] = jnp.zeros((WIDE - F, wt_ref.shape[2]), wt_ref.dtype)
        for c in range(count):
            real = ext(m_ref[0, t, c].astype(jnp.float32))
            imag = ext(m_ref[1, t, c].astype(jnp.float32))
            top = real + pltpu.roll(-imag, P_SIZE, 1)
            bottom = imag + pltpu.roll(real, P_SIZE, 1)
            base = c * WIDE
            wt_ref[t, 0:P_SIZE, base:base + WIDE] = top.astype(wt_ref.dtype)
            wt_ref[t, P_SIZE:F, base:base + WIDE] = bottom.astype(wt_ref.dtype)


def class_pieces(fixed, rows):
    low = min(fixed)
    base = sum(v << p for p, v in fixed.items())
    free = [p for p in range(rows.bit_length() - 1) if p not in fixed]
    if (1 << low) >= 8:
        outer = [p for p in free if p > low]
        starts = []
        for k in range(1 << len(outer)):
            starts.append(base + sum(((k >> i) & 1) << p for i, p in enumerate(outer)))
        return [pl.ds(st, 1 << low) for st in starts]
    above = [p for p in fixed if p > low]
    top = min(above) if above else rows.bit_length() - 1
    inner = [p for p in free if low < p < top]
    outer = [p for p in free if p < low or p > top]
    slices = []
    for k in range(1 << len(outer)):
        st = base + sum(((k >> i) & 1) << p for i, p in enumerate(outer))
        slices.append(pl.ds(st, 1 << len(inner), stride=1 << (low + 1)))
    return slices


def load_class(ref, fixed):
    chunks, rows = ref.shape[:2]
    pieces = []
    for s in class_pieces(fixed, rows):
        parts = [ref[q, s, :] for q in range(chunks)]
        pieces.append(jnp.concatenate(parts, 1))
    return pieces[0] if len(pieces) == 1 else jnp.concatenate(pieces, 0)


def store_class(ref, fixed, value):
    chunks, rows = ref.shape[:2]
    at = 0
    for s in class_pieces(fixed, rows):
        size = s.size
        for q in range(chunks):
            ref[q, s, :] = value[at:at + size, q * 128:(q + 1) * 128]
        at += size


def class_bits(bits, c):
    if len(bits) == 2:
        return {bits[0]: c >> 1, bits[1]: c & 1}
    return {bits[0]: c}


def levels_kernel(levels, packed_in, x_ref, f_ref, *refs):
    count_w = (len(refs) - 5) // 2
    m_refs = refs[:count_w]
    o_ref, s0, s1, cos_ref, sin_ref = refs[count_w:count_w + 5]
    w_refs = refs[count_w + 5:]
    build_tables(cos_ref, sin_ref, f_ref)
    for w_ref, m_ref in zip(w_refs, m_refs):
        build_weights(w_ref, m_ref)
    rows = s0.shape[1]
    block = rows // 4
    if packed_in:
        lane = lax.broadcasted_iota(jnp.int32, (block, WIDE), 1)
        parts = []
        for r in range(2):
            v = x_ref[:, r, :].astype(jnp.float32)
            parts.append(jnp.concatenate([v, jnp.zeros((block, 640 - 4 * P_SIZE), jnp.float32)], 1))
        for b in range(4):
            re = pltpu.roll(parts[0], (640 - b * P_SIZE) % 640, 1)[:, :WIDE]
            im = pltpu.roll(parts[1], (640 + P_SIZE - b * P_SIZE) % 640, 1)[:, :WIDE]
            piece = jnp.where(lane < P_SIZE, re, jnp.where(lane < F, im, 0.0))
            for q in range(WIDE // 128):
                s0[q, b * block:(b + 1) * block, :] = piece[:, q * 128:(q + 1) * 128]
    else:
        v = x_ref[...].astype(jnp.float32)
        v = jnp.concatenate([v, jnp.zeros((WIDE - F, rows), jnp.float32)], 0).T
        for q in range(WIDE // 128):
            s0[q] = v[:, q * 128:(q + 1) * 128]
    bufs = (s0, s1)
    for index, (kind, bits) in enumerate(levels):
        src = bufs[index % 2]
        dst = bufs[(index + 1) % 2]
        count = 4 if kind == "quad" else 2
        w_ref = w_refs[0] if kind == "quad" else w_refs[-1]
        children = [load_class(src, class_bits(bits, c)).astype(jnp.bfloat16) for c in range(count)]
        stacked = jnp.concatenate(children, 1)
        for t in range(count):
            fixed = class_bits(bits, t)
            y = lax.dot_general(
                stacked, w_ref[t], (((1,), (1,)), ((), ())), preferred_element_type=jnp.float32
            )
            lane = lax.broadcasted_iota(jnp.int32, y.shape, 1)
            swapped = jnp.where(lane < P_SIZE, pltpu.roll(y, WIDE - P_SIZE, 1), pltpu.roll(y, P_SIZE, 1))
            cs = load_class(cos_ref, fixed)
            sn = load_class(sin_ref, fixed)
            out = (y * cs + swapped * sn).astype(jnp.bfloat16).astype(jnp.float32)
            store_class(dst, fixed, out)
    last = bufs[len(levels) % 2]
    lane = lax.broadcasted_iota(jnp.int32, (block, 640), 1)
    pad = jnp.zeros((block, 640 - WIDE), jnp.float32)
    totals = [None, None]
    for b in range(4):
        piece = jnp.concatenate([last[q, b * block:(b + 1) * block, :] for q in range(WIDE // 128)], 1)
        piece = jnp.concatenate([piece, pad], 1)
        re = jnp.where(lane < P_SIZE, piece, 0.0)
        im = jnp.where((lane >= P_SIZE) & (lane < F), piece, 0.0)
        if b:
            re = pltpu.roll(re, b * P_SIZE, 1)
        im = pltpu.roll(im, (640 + b * P_SIZE - P_SIZE) % 640, 1)
        totals[0] = re if totals[0] is None else totals[0] + re
        totals[1] = im if totals[1] is None else totals[1] + im
    for r in range(2):
        o_ref[:, r, :] = totals[r][:, :4 * P_SIZE].astype(o_ref.dtype)


def run_levels(levels, packed_in, x, f_t, m_list):
    rows = 1024
    vmem = pl.BlockSpec(memory_space=pltpu.VMEM)
    w_scratch = [
        pltpu.VMEM((m.shape[1], WIDE, m.shape[2] * WIDE), jnp.bfloat16) for m in m_list
    ]
    m_list = [jnp.pad(m, [(0, 0)] * 4 + [(0, LANE - P_SIZE)]) for m in m_list]
    return pl.pallas_call(
        functools.partial(levels_kernel, levels, packed_in),
        out_shape=jax.ShapeDtypeStruct((rows // 4, 2, 4 * P_SIZE), jnp.bfloat16),
        in_specs=[vmem] * (2 + len(m_list)),
        out_specs=vmem,
        scratch_shapes=[pltpu.VMEM((WIDE // 128, rows, 128), jnp.float32)] * 4 + w_scratch,
        compiler_params=pltpu.CompilerParams(vmem_limit_bytes=60 * 1024 * 1024),
    )(x, f_t, *m_list)


def bits_of(value, count):
    return [(value >> k) & 1 for k in range(count)]


def factors(slope, a, b):
    center_x = (a.astype(jnp.float32) + 0.5) / 256.0 - 0.5
    center_y = (b.astype(jnp.float32) + 0.5) / 1024.0 - 0.5
    part_a = slope[0][None, :] * center_x[:, None]
    part_b = slope[1][None, :] * center_y[:, None]
    pad = [(0, 0), (0, WIDE - F)]

    def lanes(v):
        return jnp.pad(jnp.concatenate([v, v], 1), pad)

    return jnp.stack([lanes(jnp.cos(part_a)), lanes(jnp.sin(part_a)), lanes(jnp.cos(part_b)), lanes(jnp.sin(part_b))])


def build_tables(cos_ref, sin_ref, f_ref):
    groups = f_ref.shape[1]
    cb = f_ref[2]
    sb = f_ref[3]
    lane = lax.broadcasted_iota(jnp.int32, cb.shape, 1)
    for i in range(groups):
        ca = f_ref[0, i:i + 1, :]
        sa = f_ref[1, i:i + 1, :]
        cosine = ca * cb - sa * sb
        sine = sa * cb + ca * sb
        sine = jnp.where(lane < P_SIZE, -sine, sine)
        rows = pl.ds(i * groups, groups)
        for q in range(WIDE // 128):
            cos_ref[q, rows, :] = cosine[:, q * 128:(q + 1) * 128]
            sin_ref[q, rows, :] = sine[:, q * 128:(q + 1) * 128]


def exchange(z):
    shape = z.shape
    z = z.transpose(0, 1, 4, 2, 3, 5).reshape(shape[0] * shape[1], 2, -1)
    z = lax.all_to_all(z, ("gx", "gy"), 0, 0, tiled=True)
    z = z.reshape(shape[0], shape[1], 2, 2, 2, shape[5])
    return z.transpose(0, 1, 3, 4, 2, 5)


def local(source, slope, quad, pair):
    place_x = lax.axis_index("gx")
    place_y = lax.axis_index("gy")
    wq = quad.transpose(2, 0, 1, 3).reshape(2, 4, 4, P_SIZE, P_SIZE)
    wp = pair.transpose(2, 0, 1, 3).reshape(2, 2, 2, P_SIZE, P_SIZE)
    group = jnp.arange(32, dtype=jnp.int32)

    f1 = factors(slope, place_x * 32 + group, place_y * 32 + group)
    x = source.reshape(F, 1024)
    levels1 = [("quad", (k + 5, k)) for k in range(5)]
    y1 = run_levels(levels1, False, x, f1, [wq])
    z = lax.all_to_all(y1, ("gx", "gy"), 0, 0, tiled=True)
    a2 = place_x + 8 * ((group >> 3) & 1) + 16 * ((group >> 4) & 1) + 32 * (group & 7)
    b2 = place_y + 32 * group
    f2 = factors(slope, a2, b2)
    levels2 = [("quad", (5, 0)), ("quad", (6, 1)), ("quad", (7, 2)), ("pair", (3,)), ("pair", (4,))]
    y2 = run_levels(levels2, True, z, f2, [wq, wp])
    w = lax.all_to_all(y2, ("gx", "gy"), 0, 0, tiled=True)
    w = w.reshape(256, 2, 4, P_SIZE).transpose(1, 3, 2, 0)
    return w.reshape(F, 1, 1, 1024)


def solution(mesh):
    in_specs = (P(None, "gx", "gy", None), P(), P(), P())
    out_specs = P(None, "gx", "gy", None)
    return jax.shard_map(local, mesh=mesh, in_specs=in_specs, out_specs=out_specs, check_vma=False)
```
